32 devices in a mesh: seq: 8 (over y, x, core), head: 4 (over z).
Axes of the slice: x: 2, y: 2, z: 4, core: 2. Of those that a mesh axis runs over, the one named last changes fastest.
Arguments:
- query_rows: bfloat16 [1024, 2304], P(('seq', 'head')), may hold values from -6 to 6
- key_rows: bfloat16 [1024, 2304], P(('seq', 'head')), may hold values from -6 to 6
- value_rows: bfloat16 [1024, 2304], P(('seq', 'head')), may hold values from -6 to 6
- residual_in: bfloat16 [1024, 2304], P(('seq', 'head')), may hold values from -40 to 40
- norm_gain: float32 [2304], replicated, may hold values from 0.1 to 1.9
- router_weight: bfloat16 [2304, 8], replicated, may hold values from -0.125 to 0.125
- segment_ids: int32 [1024], P('seq'), may hold values from 0 to 3, never falling along the last dimension, each value on 1 to 897 neighbouring positions
- expert_ids: int32 [1024, 2], P(('seq', 'head')), may hold values from 0 to 7, all different within a row; in each aligned block of 32 rows (0 to 31, 32 to 63, ...) at most 9 rows name the same one
- gate_weight: bfloat16 [2304, 23040], P(None, ('seq', 'head')), may hold values from -0.125 to 0.125
- up_weight: bfloat16 [2304, 23040], P(None, ('seq', 'head')), may hold values from -0.125 to 0.125
- down_weight: bfloat16 [2304, 23040], P(None, ('seq', 'head')), may hold values from -0.109375 to 0.109375
- out_weight: bfloat16 [2304, 2304], P('head'), may hold values from -0.125 to 0.125
Outputs:
- residual_out: bfloat16 [1024, 2304], P(('seq', 'head'))
- key_cache: bfloat16 [1024, 2304], P('seq', 'head')
- value_cache: bfloat16 [1024, 2304], P('seq', 'head')
The draws below stay inside these ranges and needn't reach their ends.
Inputs may be any that keep to these rules, and one draw needn't show every extreme that they name: `segment_ids`: each segment covers at most 897 tokens. `expert_ids`: in the rows of one device no expert is named more than 9 times.
All inputs are finite; a program needn't handle non-finite values.
Results may differ from the reference program's by a relative error of at most 0.005.
Values may be sent and summed in bfloat16 or wider, within the bound.
No kernel may reach another device: no remote copies, remote signals or barrier semaphores. Data moves between devices by JAX's collectives and lax.ppermute only.
A program may use at most 128 MiB of HBM per device.

```python
import math
import jax
import jax.numpy as jnp
import numpy as np
from jax import lax

D = 2304
HEADS = 36
HDIM = 64
EXPERTS = 8
TOPK = 2
FFE = 2880
TOK_DEV = 32
QW = 2304
STRETCH = 128
TOKENS = 1024
SPAN = 8
MAXLEN = 897
SEGMENTS = 4
CAP = 9
GROUP = 1
HID = 2880
N_SEQ = 8
N_HEAD = 4


def drawn_pair(key):
    shape = (TOKENS, HEADS, HDIM)
    query_base = jnp.clip(jax.random.normal(jax.random.fold_in(key, 11), shape, jnp.float32), -6.0, 6.0)
    key_base = jnp.clip(jax.random.normal(jax.random.fold_in(key, 12), shape, jnp.float32), -6.0, 6.0)
    return (query_base.reshape(TOKENS, HEADS * HDIM), key_base.reshape(TOKENS, HEADS * HDIM))


def draw_query_rows(key, part):
    return drawn_pair(key)[0].astype(jnp.bfloat16)


def draw_key_rows(key, part):
    return drawn_pair(key)[1].astype(jnp.bfloat16)


def draw_residual_in(key, part):
    low = math.log(0.3)
    high = math.log(3.0)
    row_scale = jnp.exp(jax.random.uniform(jax.random.fold_in(key, 21), (TOKENS, 1), jnp.float32, low, high))
    col_scale = jnp.exp(jax.random.uniform(jax.random.fold_in(key, 22), (1, D), jnp.float32, low, high))
    noise = jnp.clip(jax.random.normal(jax.random.fold_in(key, 23), (TOKENS, D), jnp.float32), -4.0, 4.0)
    values = noise * row_scale * col_scale
    return values.astype(jnp.bfloat16)


def block_levels(rng, dims, split, low, largest):
    def one(position, blocks):
        draws = jax.random.uniform(jax.random.fold_in(jax.random.fold_in(rng, 6), position), (blocks,), jnp.float32, low / len(split), largest / len(split))
        return jnp.repeat(jnp.exp(draws), dims[position] // blocks).reshape((-1,) + (1,) * (len(dims) - position - 1))

    factor_of = one(*split[0])
    for cut in split[1:]:
        factor_of = factor_of * one(*cut)
    return factor_of


def profile(amount, total, most, skew):
    weights = [(1 << 20) // math.isqrt(standing ** skew) + 1 for standing in range(2, amount + 1)]
    rest, given = total - most - (amount - 1), [1] * (amount - 1)
    while rest > 0:
        free = [i for i in range(amount - 1) if given[i] < most]
        mass, budget = sum([weights[i] for i in free]), rest
        for i in free:
            addition = min(most - given[i], max(1, budget * weights[i] // mass), rest)
            given[i] = given[i] + addition
            rest = rest - addition
    return np.array([most] + given)


def ragged(key, amount, total, reach, lean):
    if amount == 2:
        one = jax.random.randint(key, (), max(1, total - reach), min(reach, total - 1) + 1)
        return jnp.stack([one, total - one])
    tallies = jnp.asarray(profile(amount, total, reach, lean), jnp.int32)
    couples = (amount - 1) // 2
    source_of, sink = tallies[1:1 + 2 * couples:2], tallies[2:2 + 2 * couples:2]
    margin = jnp.minimum(source_of - 1, reach - sink)
    moved = jax.random.randint(jax.random.fold_in(key, 1), (couples,), 0, 1 << 20) % (margin + 1)
    tallies = tallies.at[1:1 + 2 * couples:2].set(source_of - moved).at[2:2 + 2 * couples:2].set(sink + moved)
    return tallies[jax.random.permutation(jax.random.fold_in(key, 2), amount)]


def shared_out(rng, own, number, rows, number_of, top, most, lean):
    sequence = jax.random.permutation(rng, number_of)
    packed, ordinary = portions_of(number_of, rows * top, most, lean, True), portions_of(number_of, rows * top, most, lean, False)
    places = jnp.arange(number_of)

    def named(lengths, offset_by):
        used = int((lengths > 0).sum())
        fixed = max(1, used // 4)
        shifted = fixed + (places - fixed + offset_by * (used - fixed)) % max(1, number_of - fixed)
        return jnp.zeros((number_of,), jnp.int32).at[sequence[jnp.where(places < fixed, places, shifted)]].set(jnp.asarray(lengths, jnp.int32))

    lengths = jnp.where(number % 4 == 0, named(packed, number // 4), named(ordinary, number - number // 4 - 1))
    mixed = jax.random.permutation(jax.random.fold_in(own, 3), number_of)
    giver, sink = mixed[0:number_of // 2 * 2:2], mixed[1:number_of // 2 * 2:2]
    room = jnp.minimum(lengths[giver] - 1, most - lengths[sink]) // 2
    room = jnp.where((giver == sequence[0]) | (sink == sequence[0]) | (lengths[sink] == 0), 0, jnp.maximum(room, 0))
    shifted = jax.random.randint(jax.random.fold_in(own, 4), (number_of // 2,), 0, 1 << 20) % (room + 1)
    lengths = lengths.at[giver].add(-shifted).at[sink].add(shifted)
    items = jnp.searchsorted(jnp.cumsum(lengths), jnp.arange(rows * top), side="right").astype(jnp.int32)
    listing = items.reshape(top, rows).T
    listing = listing[jax.random.permutation(jax.random.fold_in(own, 1), rows)]
    offset_by = jax.random.randint(jax.random.fold_in(own, 2), (rows, 1), 0, top)
    return jnp.take_along_axis(listing, (jnp.arange(top)[None, :] + offset_by) % top, axis=1)


def portions_of(count, total, most, skew, full):
    loads = [(1 << 20) // math.isqrt(grade ** skew) + 1 for grade in range(1, count + 1)]
    largest = most if full else min(most, max(-(-total // count), total * loads[0] // sum(loads)))
    least = 1 if total - largest >= count - 1 else 0
    holding, surplus = [largest] + [least] * (count - 1), total - largest - least * (count - 1)
    while surplus > 0:
        movable = [i for i in range(1, count) if holding[i] < largest] or [i for i in range(1, count) if holding[i] < most]
        whole, left = sum([loads[i] for i in movable]), surplus
        for i in movable:
            addition = min(most - holding[i], max(1, left * loads[i] // whole), surplus)
            holding[i] = holding[i] + addition
            surplus = surplus - addition
    return np.array(holding)


def scatter_about(key, dims, scale, most, pieces=(), kind=jnp.bfloat16):
    array = scale * jax.random.normal(key, dims, jnp.float32)
    if pieces:
        array = array * block_levels(key, dims, pieces, -0.22, 0.18)
    return jnp.clip(array, -most, most).astype(kind)


def setup_inputs(seed: int = 0) -> dict:
    key_list = jax.random.split(jax.random.key(seed), 13)
    query_rows = draw_query_rows(jax.random.fold_in(key_list[12], 71), 0)
    key_rows = draw_key_rows(jax.random.fold_in(key_list[12], 71), 0)
    value_rows = scatter_about(key_list[2], (TOKENS, QW), 1.0, 6.0, ((0, 32),))
    residual_in = draw_residual_in(jax.random.fold_in(key_list[12], 71), 0)
    norm_gain = jnp.clip(1.0 + 0.18 * jax.random.normal(key_list[4], (D,), jnp.float32), 0.1, 1.9)
    router_weight = scatter_about(key_list[5], (D, EXPERTS), D ** -0.5, 0.125)
    segment_ids = jnp.searchsorted(jnp.cumsum(ragged(key_list[6], SEGMENTS, TOKENS, MAXLEN, 3)), jnp.arange(TOKENS), side="right").astype(jnp.int32)
    expert_ids_keys = jax.random.split(jax.random.fold_in(key_list[7], 1), TOKENS // TOK_DEV)
    expert_ids_turns = jax.random.permutation(jax.random.fold_in(key_list[7], 3), TOKENS // TOK_DEV)
    expert_ids = jax.vmap(lambda own, number: shared_out(jax.random.fold_in(key_list[7], 2), own, number, TOK_DEV, EXPERTS, TOPK, CAP, 1))(expert_ids_keys, expert_ids_turns).reshape((TOKENS, TOPK))
    gate_weight = scatter_about(key_list[8], (D, EXPERTS * FFE), D ** -0.5, 0.125, ((1, 32),))
    up_weight = scatter_about(key_list[9], (D, EXPERTS * FFE), D ** -0.5, 0.125, ((1, 32),))
    down_weight = scatter_about(key_list[10], (D, EXPERTS * FFE), FFE ** -0.5, 0.109375, ((1, 32),))
    out_weight = scatter_about(key_list[11], (QW, D), QW ** -0.5, 0.125, ((0, 4),))
    return {"query_rows": query_rows, "key_rows": key_rows, "value_rows": value_rows, "residual_in": residual_in, "norm_gain": norm_gain, "router_weight": router_weight, "segment_ids": segment_ids, "expert_ids": expert_ids, "gate_weight": gate_weight, "up_weight": up_weight, "down_weight": down_weight, "out_weight": out_weight}


residual_scale = 1.4 / math.sqrt(40.0)
norm_epsilon = 1e-05

def attend_block(block_index, query_rows, key_pad, value_pad, segment_ids, segment_pad):
    offset_start = (block_index * STRETCH).astype(jnp.int32)
    window_len = SPAN * STRETCH
    queries = lax.dynamic_slice_in_dim(query_rows, offset_start, STRETCH, 0).reshape(STRETCH, HEADS, HDIM).astype(jnp.float32)
    keys_all = lax.dynamic_slice_in_dim(key_pad, offset_start, window_len, 0).reshape(window_len, HEADS, HDIM).astype(jnp.float32)
    values_all = lax.dynamic_slice_in_dim(value_pad, offset_start, window_len, 0).reshape(window_len, HEADS, HDIM).astype(jnp.float32)
    query_segment = lax.dynamic_slice_in_dim(segment_ids, offset_start, STRETCH, 0)
    key_segment = lax.dynamic_slice_in_dim(segment_pad, offset_start, window_len, 0)
    query_place = offset_start + jnp.arange(STRETCH, dtype=jnp.int32)
    key_place = offset_start - (SPAN - 1) * STRETCH + jnp.arange(window_len, dtype=jnp.int32)
    allowed = (key_segment[None, :] == query_segment[:, None]) & (key_place[None, :] <= query_place[:, None]) & (key_place[None, :] >= 0)
    scores = jnp.einsum('qhd,khd->hqk', queries, keys_all) * HDIM ** (-0.5)
    masked = jnp.where(allowed[None], scores, -jnp.inf)
    row_max = lax.optimization_barrier(jnp.max(masked, -1, keepdims=True))
    weights = jnp.where(allowed[None], jnp.exp(masked - row_max), 0.0)
    totals = lax.optimization_barrier(jnp.sum(weights, -1))
    rounded = lax.optimization_barrier(weights.astype(jnp.bfloat16)).astype(jnp.float32)
    mixture = jnp.einsum('hqk,khd->qhd', rounded, values_all)
    mixture = mixture / jnp.transpose(totals)[:, :, None]
    return mixture.reshape(STRETCH, QW).astype(jnp.bfloat16)

def reference(query_rows, key_rows, value_rows, residual_in, norm_gain, router_weight, segment_ids, expert_ids, gate_weight, up_weight, down_weight, out_weight):
    front = (SPAN - 1) * STRETCH
    key_pad = jnp.concatenate((jnp.zeros((front, QW), jnp.bfloat16), key_rows), 0)
    value_pad = jnp.concatenate((jnp.zeros((front, QW), jnp.bfloat16), value_rows), 0)
    segment_pad = jnp.concatenate((jnp.full((front,), -1, jnp.int32), segment_ids), 0)

    def one_block(block_index):
        return attend_block(block_index, query_rows, key_pad, value_pad, segment_ids, segment_pad)
    attention = lax.map(one_block, jnp.arange(N_SEQ, dtype=jnp.int32)).reshape(TOKENS, QW)
    attended_sum = jnp.dot(attention, out_weight, preferred_element_type=jnp.float32)
    middle = (residual_in.astype(jnp.float32) + residual_scale * attended_sum).astype(jnp.bfloat16)
    middle_wide = middle.astype(jnp.float32)
    mean_square = lax.optimization_barrier(jnp.mean(middle_wide * middle_wide, -1, keepdims=True))
    normed = (middle_wide * lax.rsqrt(mean_square + norm_epsilon) * norm_gain.astype(jnp.float32)).astype(jnp.bfloat16)
    logits = jnp.dot(normed, router_weight, preferred_element_type=jnp.float32)
    chosen = jnp.take_along_axis(logits, expert_ids, 1)
    first_weight = 1.0 / (1.0 + jnp.exp(chosen[:, 1] - chosen[:, 0]))
    second_weight = 1.0 / (1.0 + jnp.exp(chosen[:, 0] - chosen[:, 1]))
    route_weight = jnp.stack((first_weight, second_weight), 1)
    bound = min(TOKENS, N_SEQ * N_HEAD * CAP)

    def expert_step(accumulated, expert):
        picked = expert_ids == expert
        member_mask = jnp.any(picked, 1)
        route_share = lax.optimization_barrier(jnp.sum(jnp.where(picked, route_weight, 0.0), 1))
        positions = jnp.nonzero(member_mask, size=bound, fill_value=0)[0].astype(jnp.int32)
        filled = jnp.arange(bound, dtype=jnp.int32) < jnp.sum(member_mask.astype(jnp.int32))
        token_rows = normed[positions]
        column = (expert * FFE).astype(jnp.int32)
        gate_cols = lax.dynamic_slice_in_dim(gate_weight, column, FFE, 1)
        up_cols = lax.dynamic_slice_in_dim(up_weight, column, FFE, 1)
        down_cols = lax.dynamic_slice_in_dim(down_weight, column, FFE, 1)
        gate_act = jnp.dot(token_rows, gate_cols, preferred_element_type=jnp.float32)
        up_act = jnp.dot(token_rows, up_cols, preferred_element_type=jnp.float32)
        hidden = (jax.nn.silu(gate_act) * up_act).astype(jnp.bfloat16)

        def shard_step(running, shard_index):
            shard_start = (shard_index * HID).astype(jnp.int32)
            part_hidden = lax.dynamic_slice_in_dim(hidden, shard_start, HID, 1)
            part_down = lax.dynamic_slice_in_dim(down_cols, shard_start, HID, 1)
            product = lax.dot_general(part_hidden, part_down, (((1,), (1,)), ((), ())), preferred_element_type=jnp.float32)
            product = lax.optimization_barrier(product.astype(jnp.bfloat16)).astype(jnp.float32)
            return (running + product, None)
        expert_out, unused_rest = lax.scan(shard_step, jnp.zeros((bound, D), jnp.float32), jnp.arange(GROUP, dtype=jnp.int32))
        share_rows = jnp.where(filled, route_share[positions], 0.0)
        accumulated = accumulated.at[positions].add(expert_out * share_rows[:, None])
        return (accumulated, None)
    moe_sum, unused_tail = lax.scan(expert_step, jnp.zeros((TOKENS, D), jnp.float32), jnp.arange(EXPERTS, dtype=jnp.int32))
    residual_out = (middle_wide + residual_scale * moe_sum).astype(jnp.bfloat16)
    return (residual_out, key_rows, value_rows)
```

```python
import math

import jax
import jax.numpy as jnp
from jax import lax
from jax.sharding import PartitionSpec as P

D = 2304
HDIM = 64
LEVELS = 4
CAP = 9


residual_scale = 1.4 / math.sqrt(40.0)
norm_epsilon = 1e-05


def passed_along(value, axis, by):
    length = lax.axis_size(axis)
    pairs = [(i, i + by) for i in range(length) if 0 <= i + by < length]
    return lax.ppermute(value, axis, pairs)


def score_piece(queries, key_piece, piece_allowed):
    raw_scores = jnp.einsum(
        "qhd,khd->hqk", queries, key_piece, preferred_element_type=jnp.float32
    ) * queries.shape[2] ** (-0.5)
    return jnp.where(piece_allowed[None], raw_scores, -jnp.inf)


def mix_piece(rounded_piece, value_piece):
    return jnp.einsum(
        "hqk,khd->qhd", rounded_piece, value_piece, preferred_element_type=jnp.float32
    )


def per_device(
    query_rows,
    key_rows,
    value_rows,
    residual_in,
    norm_gain,
    router_weight,
    segment_ids,
    expert_ids,
    gate_weight,
    up_weight,
    down_weight,
    out_weight,
):
    head_count = lax.axis_size("head")
    seq_count = lax.axis_size("seq")
    tok_local = query_rows.shape[0]
    group_width = query_rows.shape[1] // head_count
    heads_here = group_width // HDIM
    stretch_len = tok_local * head_count
    span_count = min(2**LEVELS * 32 // tok_local, seq_count)
    expert_count = router_weight.shape[1]
    replicas = seq_count // expert_count
    seq_place = lax.axis_index("seq")
    query_head, key_head, value_head = (
        lax.all_to_all(
            query_rows.reshape(tok_local, head_count, group_width),
            "head",
            split_axis=1,
            concat_axis=0,
            tiled=True,
        ),
        lax.all_to_all(
            key_rows.reshape(tok_local, head_count, group_width),
            "head",
            split_axis=1,
            concat_axis=0,
            tiled=True,
        ),
        lax.all_to_all(
            value_rows.reshape(tok_local, head_count, group_width),
            "head",
            split_axis=1,
            concat_axis=0,
            tiled=True,
        ),
    )
    query_head = query_head.reshape(stretch_len, group_width)
    key_head = key_head.reshape(stretch_len, group_width)
    value_head = value_head.reshape(stretch_len, group_width)
    front_rows = (span_count - 1) * stretch_len
    key_window = jnp.concatenate((jnp.zeros((front_rows, group_width), jnp.bfloat16), key_head), 0)
    value_window = jnp.concatenate(
        (jnp.zeros((front_rows, group_width), jnp.bfloat16), value_head), 0
    )
    segment_window = jnp.concatenate((jnp.zeros((front_rows,), jnp.int32), segment_ids), 0)

    def advance(step_index, carried):
        moving, keys_held, values_held, segments_held = carried
        moving = passed_along((moving[0], moving[1], moving[2]), "seq", 1)
        write_place = (span_count - 1 - step_index) * stretch_len
        keys_held = lax.dynamic_update_slice_in_dim(keys_held, moving[0], write_place, 0)
        values_held = lax.dynamic_update_slice_in_dim(values_held, moving[1], write_place, 0)
        segments_held = lax.dynamic_update_slice_in_dim(segments_held, moving[2], write_place, 0)
        return (moving, keys_held, values_held, segments_held)

    moving_final, key_window, value_window, segment_window = lax.fori_loop(
        1,
        span_count,
        advance,
        ((key_head, value_head, segment_ids), key_window, value_window, segment_window),
    )
    key_total = span_count * stretch_len
    query_place = seq_place * stretch_len + jnp.arange(stretch_len, dtype=jnp.int32)
    key_place = (seq_place - span_count + 1) * stretch_len + jnp.arange(key_total, dtype=jnp.int32)
    allowed = (
        (segment_window[None, :] == segment_ids[:, None])
        & (key_place[None, :] <= query_place[:, None])
        & (key_place[None, :] >= 0)
    )
    queries = query_head.reshape(stretch_len, heads_here, HDIM)
    keys_all = key_window.reshape(key_total, heads_here, HDIM)
    values_all = value_window.reshape(key_total, heads_here, HDIM)
    masked = score_piece(queries, keys_all, allowed)
    row_max = jnp.max(masked, -1, keepdims=True)
    weights = jnp.where(allowed[None], jnp.exp(masked - row_max), 0.0)
    totals = jnp.sum(weights, -1)
    mixture = mix_piece(weights.astype(jnp.bfloat16), values_all)
    attention = (
        (mixture / jnp.transpose(totals)[:, :, None])
        .astype(jnp.bfloat16)
        .reshape(stretch_len, group_width)
    )
    attended_sum = lax.psum_scatter(
        jnp.dot(attention, out_weight, preferred_element_type=jnp.float32).astype(jnp.bfloat16),
        "head",
        scatter_dimension=0,
        tiled=True,
    ).astype(jnp.float32)
    middle = (residual_in.astype(jnp.float32) + residual_scale * attended_sum).astype(jnp.bfloat16)
    middle_wide = middle.astype(jnp.float32)
    mean_square = jnp.mean(middle_wide * middle_wide, -1, keepdims=True)
    normed = (middle_wide * lax.rsqrt(mean_square + norm_epsilon) * norm_gain).astype(jnp.bfloat16)
    route_count = expert_ids.shape[1]
    logits = jnp.dot(normed, router_weight, preferred_element_type=jnp.float32)
    route_hot = expert_ids[:, :, None] == jnp.arange(expert_count, dtype=jnp.int32)[None, None, :]
    chosen = jnp.sum(jnp.where(route_hot, logits[:, None, :], 0.0), -1)
    first_weight = 1.0 / (1.0 + jnp.exp(chosen[:, 1] - chosen[:, 0]))
    second_weight = 1.0 / (1.0 + jnp.exp(chosen[:, 0] - chosen[:, 1]))
    flat_hot = route_hot.reshape(tok_local * route_count, expert_count).astype(jnp.int32)
    before_count = jnp.cumsum(flat_hot, 0) - flat_hot
    route_rank = jnp.sum(before_count * flat_hot, -1)
    slot_ids = (expert_ids.reshape(-1) * CAP + route_rank).reshape(tok_local, route_count)
    slot_total = expert_count * CAP
    dispatch = jnp.any(
        slot_ids[None, :, :] == jnp.arange(slot_total, dtype=jnp.int32)[:, None, None], -1
    ).astype(jnp.bfloat16)
    packed = (
        jnp.dot(dispatch, normed, preferred_element_type=jnp.float32)
        .astype(jnp.bfloat16)
        .reshape(expert_count, CAP, D)
    )
    outgoing = jnp.broadcast_to(packed[:, None], (expert_count, replicas, CAP, D)).reshape(
        seq_count, CAP, D
    )
    arrived = lax.all_to_all(outgoing, "seq", split_axis=0, concat_axis=0, tiled=True)
    slot_count = arrived.shape[1]
    flat_rows = arrived.reshape(seq_count * slot_count, D)
    group_rows = lax.all_gather(flat_rows, "head", axis=0, tiled=True)
    gate_act = jnp.dot(group_rows, gate_weight, preferred_element_type=jnp.float32)
    up_act = jnp.dot(group_rows, up_weight, preferred_element_type=jnp.float32)
    hidden = (jax.nn.silu(gate_act) * up_act).astype(jnp.bfloat16)
    partial_out = lax.dot_general(
        hidden, down_weight, (((1,), (1,)), ((), ())), preferred_element_type=jnp.float32
    )
    shard_out = lax.psum_scatter(partial_out, "head", scatter_dimension=0, tiled=True).astype(
        jnp.bfloat16
    )
    returned = lax.all_to_all(
        shard_out.reshape(seq_count, slot_count, D), "seq", split_axis=0, concat_axis=0, tiled=True
    )
    expert_out = jnp.sum(
        returned.reshape(expert_count, replicas, CAP, D).astype(jnp.float32), 1
    ).reshape(slot_total, D)
    first_rows = expert_out[slot_ids[:, 0]]
    second_rows = expert_out[slot_ids[:, 1]]
    moe_sum = first_weight[:, None] * first_rows + second_weight[:, None] * second_rows
    residual_out = (middle_wide + residual_scale * moe_sum).astype(jnp.bfloat16)
    return (residual_out, key_head, value_head)


def solution(mesh):
    return jax.shard_map(
        per_device,
        mesh=mesh,
        in_specs=(
            P(("seq", "head"), None),
            P(("seq", "head"), None),
            P(("seq", "head"), None),
            P(("seq", "head"), None),
            P(),
            P(),
            P("seq"),
            P(("seq", "head"), None),
            P(None, ("seq", "head")),
            P(None, ("seq", "head")),
            P(None, ("seq", "head")),
            P("head", None),
        ),
        out_specs=(P(("seq", "head"), None), P("seq", "head"), P("seq", "head")),
        check_vma=False,
    )
```

```python
import math

import jax
import jax.numpy as jnp
from jax import lax
from jax.sharding import PartitionSpec as P

D = 2304
HDIM = 64
LEVELS = 4
CAP = 9


residual_scale = 1.4 / math.sqrt(40.0)
norm_epsilon = 1e-05


def passed_along(value, axis, by):
    length = lax.axis_size(axis)
    pairs = [(i, i + by) for i in range(length) if 0 <= i + by < length]
    return lax.ppermute(value, axis, pairs)


def score_piece(queries, key_piece, piece_allowed):
    raw_scores = jnp.einsum(
        "qhd,khd->hqk", queries, key_piece, preferred_element_type=jnp.float32
    ) * queries.shape[2] ** (-0.5)
    return jnp.where(piece_allowed[None], raw_scores, -jnp.inf)


def mix_piece(rounded_piece, value_piece):
    return jnp.einsum(
        "hqk,khd->qhd", rounded_piece, value_piece, preferred_element_type=jnp.float32
    )


def per_device(
    query_rows,
    key_rows,
    value_rows,
    residual_in,
    norm_gain,
    router_weight,
    segment_ids,
    expert_ids,
    gate_weight,
    up_weight,
    down_weight,
    out_weight,
):
    head_count = lax.axis_size("head")
    seq_count = lax.axis_size("seq")
    tok_local = query_rows.shape[0]
    group_width = query_rows.shape[1] // head_count
    heads_here = group_width // HDIM
    stretch_len = tok_local * head_count
    span_count = min(2**LEVELS * 32 // tok_local, seq_count)
    expert_count = router_weight.shape[1]
    replicas = seq_count // expert_count
    seq_place = lax.axis_index("seq")
    stacked = jnp.stack(
        (
            query_rows.reshape(tok_local, head_count, group_width),
            key_rows.reshape(tok_local, head_count, group_width),
            value_rows.reshape(tok_local, head_count, group_width),
        ),
        2,
    )
    by_head = lax.all_to_all(stacked, "head", split_axis=1, concat_axis=0, tiled=True)
    query_head = by_head[:, 0, 0]
    key_head = by_head[:, 0, 1]
    value_head = by_head[:, 0, 2]
    joined_head = by_head[:, 0, 1:].reshape(stretch_len, 2 * group_width)
    pieces = [joined_head]
    for distance in range(1, span_count):
        pieces.append(passed_along(joined_head, "seq", distance))
    joined_window = jnp.concatenate(pieces[::-1], 0)
    key_window = joined_window[:, :group_width]
    value_window = joined_window[:, group_width:]
    front_rows = (span_count - 1) * stretch_len
    all_segments = lax.all_gather(segment_ids, "seq", axis=0, tiled=True)
    segment_window = lax.dynamic_slice_in_dim(
        jnp.concatenate((jnp.zeros((front_rows,), jnp.int32), all_segments), 0),
        seq_place * stretch_len,
        span_count * stretch_len,
        0,
    )
    key_total = span_count * stretch_len
    query_place = seq_place * stretch_len + jnp.arange(stretch_len, dtype=jnp.int32)
    key_place = (seq_place - span_count + 1) * stretch_len + jnp.arange(key_total, dtype=jnp.int32)
    allowed = (
        (segment_window[None, :] == segment_ids[:, None])
        & (key_place[None, :] <= query_place[:, None])
        & (key_place[None, :] >= 0)
    )
    queries = query_head.reshape(stretch_len, heads_here, HDIM)
    keys_all = key_window.reshape(key_total, heads_here, HDIM)
    values_all = value_window.reshape(key_total, heads_here, HDIM)
    masked = score_piece(queries, keys_all, allowed)
    row_max = jnp.max(masked, -1, keepdims=True)
    weights = jnp.where(allowed[None], jnp.exp(masked - row_max), 0.0)
    totals = jnp.sum(weights, -1)
    mixture = mix_piece(weights.astype(jnp.bfloat16), values_all)
    attention = (
        (mixture / jnp.transpose(totals)[:, :, None])
        .astype(jnp.bfloat16)
        .reshape(stretch_len, group_width)
    )
    attended_sum = lax.psum_scatter(
        jnp.dot(attention, out_weight, preferred_element_type=jnp.float32).astype(jnp.bfloat16),
        "head",
        scatter_dimension=0,
        tiled=True,
    ).astype(jnp.float32)
    middle = (residual_in.astype(jnp.float32) + residual_scale * attended_sum).astype(jnp.bfloat16)
    middle_wide = middle.astype(jnp.float32)
    mean_square = jnp.mean(middle_wide * middle_wide, -1, keepdims=True)
    normed = (middle_wide * lax.rsqrt(mean_square + norm_epsilon) * norm_gain).astype(jnp.bfloat16)
    route_count = expert_ids.shape[1]
    logits = jnp.dot(normed, router_weight, preferred_element_type=jnp.float32)
    route_hot = expert_ids[:, :, None] == jnp.arange(expert_count, dtype=jnp.int32)[None, None, :]
    chosen = jnp.sum(jnp.where(route_hot, logits[:, None, :], 0.0), -1)
    first_weight = 1.0 / (1.0 + jnp.exp(chosen[:, 1] - chosen[:, 0]))
    second_weight = 1.0 / (1.0 + jnp.exp(chosen[:, 0] - chosen[:, 1]))
    flat_hot = route_hot.reshape(tok_local * route_count, expert_count).astype(jnp.int32)
    before_count = jnp.cumsum(flat_hot, 0) - flat_hot
    route_rank = jnp.sum(before_count * flat_hot, -1)
    slot_ids = (expert_ids.reshape(-1) * CAP + route_rank).reshape(tok_local, route_count)
    slot_total = expert_count * CAP
    dispatch = jnp.any(
        slot_ids[None, :, :] == jnp.arange(slot_total, dtype=jnp.int32)[:, None, None], -1
    ).astype(jnp.bfloat16)
    packed = (
        jnp.dot(dispatch, normed, preferred_element_type=jnp.float32)
        .astype(jnp.bfloat16)
        .reshape(expert_count, CAP, D)
    )
    outgoing = jnp.broadcast_to(packed[:, None], (expert_count, replicas, CAP, D)).reshape(
        seq_count, CAP, D
    )
    arrived = lax.all_to_all(outgoing, "seq", split_axis=0, concat_axis=0, tiled=True)
    slot_count = arrived.shape[1]
    flat_rows = arrived.reshape(seq_count * slot_count, D)
    group_rows = lax.all_gather(flat_rows, "head", axis=0, tiled=True)
    gate_act = jnp.dot(group_rows, gate_weight, preferred_element_type=jnp.float32)
    up_act = jnp.dot(group_rows, up_weight, preferred_element_type=jnp.float32)
    hidden = (jax.nn.silu(gate_act) * up_act).astype(jnp.bfloat16)
    partial_out = lax.dot_general(
        hidden, down_weight, (((1,), (1,)), ((), ())), preferred_element_type=jnp.float32
    )
    shard_out = lax.psum_scatter(partial_out, "head", scatter_dimension=0, tiled=True).astype(
        jnp.bfloat16
    )
    returned = lax.all_to_all(
        shard_out.reshape(seq_count, slot_count, D), "seq", split_axis=0, concat_axis=0, tiled=True
    )
    expert_out = jnp.sum(
        returned.reshape(expert_count, replicas, CAP, D).astype(jnp.float32), 1
    ).reshape(slot_total, D)
    first_rows = expert_out[slot_ids[:, 0]]
    second_rows = expert_out[slot_ids[:, 1]]
    moe_sum = first_weight[:, None] * first_rows + second_weight[:, None] * second_rows
    residual_out = (middle_wide + residual_scale * moe_sum).astype(jnp.bfloat16)
    return (residual_out, key_head, value_head)


def solution(mesh):
    return jax.shard_map(
        per_device,
        mesh=mesh,
        in_specs=(
            P(("seq", "head"), None),
            P(("seq", "head"), None),
            P(("seq", "head"), None),
            P(("seq", "head"), None),
            P(),
            P(),
            P("seq"),
            P(("seq", "head"), None),
            P(None, ("seq", "head")),
            P(None, ("seq", "head")),
            P(None, ("seq", "head")),
            P("head", None),
        ),
        out_specs=(P(("seq", "head"), None), P("seq", "head"), P("seq", "head")),
        check_vma=False,
    )
```

```python
import math

import jax
import jax.numpy as jnp
from jax import lax
from jax.sharding import PartitionSpec as P

D = 2304
HDIM = 64
LEVELS = 4
CAP = 9


residual_scale = 1.4 / math.sqrt(40.0)
norm_epsilon = 1e-05


def passed_along(value, axis, by):
    length = lax.axis_size(axis)
    pairs = [(i, i + by) for i in range(length) if 0 <= i + by < length]
    return lax.ppermute(value, axis, pairs)


def score_piece(queries, key_piece, piece_allowed):
    raw_scores = jnp.einsum(
        "qhd,khd->hqk", queries, key_piece, preferred_element_type=jnp.float32
    ) * queries.shape[2] ** (-0.5)
    return jnp.where(piece_allowed[None], raw_scores, -jnp.inf)


def mix_piece(rounded_piece, value_piece):
    return jnp.einsum(
        "hqk,khd->qhd", rounded_piece, value_piece, preferred_element_type=jnp.float32
    )


def per_device(
    query_rows,
    key_rows,
    value_rows,
    residual_in,
    norm_gain,
    router_weight,
    segment_ids,
    expert_ids,
    gate_weight,
    up_weight,
    down_weight,
    out_weight,
):
    head_count = lax.axis_size("head")
    seq_count = lax.axis_size("seq")
    tok_local = query_rows.shape[0]
    group_width = query_rows.shape[1] // head_count
    heads_here = group_width // HDIM
    stretch_len = tok_local * head_count
    span_count = min(2**LEVELS * 32 // tok_local, seq_count)
    expert_count = router_weight.shape[1]
    replicas = seq_count // expert_count
    seq_place = lax.axis_index("seq")
    stacked = jnp.stack(
        (
            query_rows.reshape(tok_local, head_count, group_width),
            key_rows.reshape(tok_local, head_count, group_width),
            value_rows.reshape(tok_local, head_count, group_width),
        ),
        2,
    )
    by_head = lax.all_to_all(stacked, "head", split_axis=1, concat_axis=0, tiled=True)
    query_head = by_head[:, 0, 0]
    key_head = by_head[:, 0, 1]
    value_head = by_head[:, 0, 2]
    joined_head = by_head[:, 0, 1:].reshape(stretch_len, 2 * group_width)
    pieces = [joined_head]
    for distance in range(1, span_count):
        pieces.append(passed_along(joined_head, "seq", distance))
    joined_window = jnp.concatenate(pieces[::-1], 0)
    key_window = joined_window[:, :group_width]
    value_window = joined_window[:, group_width:]
    front_rows = (span_count - 1) * stretch_len
    all_segments = lax.all_gather(segment_ids, "seq", axis=0, tiled=True)
    segment_window = lax.dynamic_slice_in_dim(
        jnp.concatenate((jnp.zeros((front_rows,), jnp.int32), all_segments), 0),
        seq_place * stretch_len,
        span_count * stretch_len,
        0,
    )
    key_total = span_count * stretch_len
    query_place = seq_place * stretch_len + jnp.arange(stretch_len, dtype=jnp.int32)
    key_place = (seq_place - span_count + 1) * stretch_len + jnp.arange(key_total, dtype=jnp.int32)
    allowed = (
        (segment_window[None, :] == segment_ids[:, None])
        & (key_place[None, :] <= query_place[:, None])
        & (key_place[None, :] >= 0)
    )
    queries = query_head.reshape(stretch_len, heads_here, HDIM)
    keys_all = key_window.reshape(key_total, heads_here, HDIM)
    values_all = value_window.reshape(key_total, heads_here, HDIM)
    masked = score_piece(queries, keys_all, allowed)
    row_max = jnp.max(masked, -1, keepdims=True)
    weights = jnp.where(allowed[None], jnp.exp(masked - row_max), 0.0)
    totals = jnp.sum(weights, -1)
    mixture = mix_piece(weights.astype(jnp.bfloat16), values_all)
    attention = (
        (mixture / jnp.transpose(totals)[:, :, None])
        .astype(jnp.bfloat16)
        .reshape(stretch_len, group_width)
    )
    attended_sum = lax.psum_scatter(
        jnp.dot(attention, out_weight, preferred_element_type=jnp.float32).astype(jnp.bfloat16),
        "head",
        scatter_dimension=0,
        tiled=True,
    ).astype(jnp.float32)
    middle = (residual_in.astype(jnp.float32) + residual_scale * attended_sum).astype(jnp.bfloat16)
    middle_wide = middle.astype(jnp.float32)
    mean_square = jnp.mean(middle_wide * middle_wide, -1, keepdims=True)
    normed = (middle_wide * lax.rsqrt(mean_square + norm_epsilon) * norm_gain).astype(jnp.bfloat16)
    route_count = expert_ids.shape[1]
    logits = jnp.dot(normed, router_weight, preferred_element_type=jnp.float32)
    route_hot = expert_ids[:, :, None] == jnp.arange(expert_count, dtype=jnp.int32)[None, None, :]
    chosen = jnp.sum(jnp.where(route_hot, logits[:, None, :], 0.0), -1)
    first_weight = 1.0 / (1.0 + jnp.exp(chosen[:, 1] - chosen[:, 0]))
    second_weight = 1.0 / (1.0 + jnp.exp(chosen[:, 0] - chosen[:, 1]))
    flat_hot = route_hot.reshape(tok_local * route_count, expert_count).astype(jnp.int32)
    before_count = jnp.cumsum(flat_hot, 0) - flat_hot
    route_rank = jnp.sum(before_count * flat_hot, -1)
    slot_ids = (expert_ids.reshape(-1) * CAP + route_rank).reshape(tok_local, route_count)
    slot_total = expert_count * CAP
    dispatch = jnp.any(
        slot_ids[None, :, :] == jnp.arange(slot_total, dtype=jnp.int32)[:, None, None], -1
    ).astype(jnp.bfloat16)
    packed = (
        jnp.dot(dispatch, normed, preferred_element_type=jnp.float32)
        .astype(jnp.bfloat16)
        .reshape(expert_count, CAP, D)
    )
    outgoing = jnp.broadcast_to(packed[:, None], (expert_count, replicas, CAP, D)).reshape(
        seq_count, CAP, D
    )
    arrived = lax.all_to_all(outgoing, "seq", split_axis=0, concat_axis=0, tiled=True)
    slot_count = arrived.shape[1]
    flat_rows = arrived.reshape(seq_count * slot_count, D)
    group_rows = lax.all_gather(flat_rows, "head", axis=0, tiled=True)
    gate_act = jnp.dot(group_rows, gate_weight, preferred_element_type=jnp.float32)
    up_act = jnp.dot(group_rows, up_weight, preferred_element_type=jnp.float32)
    hidden = (jax.nn.silu(gate_act) * up_act).astype(jnp.bfloat16)
    partial_out = lax.dot_general(
        hidden, down_weight, (((1,), (1,)), ((), ())), preferred_element_type=jnp.float32
    ).astype(jnp.bfloat16)
    shard_out = lax.psum_scatter(partial_out, "head", scatter_dimension=0, tiled=True)
    returned = lax.all_to_all(
        shard_out.reshape(seq_count, slot_count, D), "seq", split_axis=0, concat_axis=0, tiled=True
    )
    expert_out = jnp.sum(
        returned.reshape(expert_count, replicas, CAP, D).astype(jnp.float32), 1
    ).reshape(slot_total, D)
    first_rows = expert_out[slot_ids[:, 0]]
    second_rows = expert_out[slot_ids[:, 1]]
    moe_sum = first_weight[:, None] * first_rows + second_weight[:, None] * second_rows
    residual_out = (middle_wide + residual_scale * moe_sum).astype(jnp.bfloat16)
    return (residual_out, key_head, value_head)


def solution(mesh):
    return jax.shard_map(
        per_device,
        mesh=mesh,
        in_specs=(
            P(("seq", "head"), None),
            P(("seq", "head"), None),
            P(("seq", "head"), None),
            P(("seq", "head"), None),
            P(),
            P(),
            P("seq"),
            P(("seq", "head"), None),
            P(None, ("seq", "head")),
            P(None, ("seq", "head")),
            P(None, ("seq", "head")),
            P("head", None),
        ),
        out_specs=(P(("seq", "head"), None), P("seq", "head"), P("seq", "head")),
        check_vma=False,
    )
```

```python
import math

import jax
import jax.numpy as jnp
from jax import lax
from jax.sharding import PartitionSpec as P

D = 2304
HDIM = 64
LEVELS = 4
CAP = 9


residual_scale = 1.4 / math.sqrt(40.0)
norm_epsilon = 1e-05


def passed_along(value, axis, by):
    length = lax.axis_size(axis)
    pairs = [(i, i + by) for i in range(length) if 0 <= i + by < length]
    return lax.ppermute(value, axis, pairs)


def score_piece(queries, key_piece, piece_allowed):
    raw_scores = jnp.einsum(
        "qhd,khd->hqk", queries, key_piece, preferred_element_type=jnp.float32
    ) * queries.shape[2] ** (-0.5)
    return jnp.where(piece_allowed[None], raw_scores, -jnp.inf)


def mix_piece(rounded_piece, value_piece):
    return jnp.einsum(
        "hqk,khd->qhd", rounded_piece, value_piece, preferred_element_type=jnp.float32
    )


def per_device(
    query_rows,
    key_rows,
    value_rows,
    residual_in,
    norm_gain,
    router_weight,
    segment_ids,
    expert_ids,
    gate_weight,
    up_weight,
    down_weight,
    out_weight,
):
    head_count = lax.axis_size("head")
    seq_count = lax.axis_size("seq")
    tok_local = query_rows.shape[0]
    group_width = query_rows.shape[1] // head_count
    heads_here = group_width // HDIM
    stretch_len = tok_local * head_count
    span_count = min(2**LEVELS * 32 // tok_local, seq_count)
    expert_count = router_weight.shape[1]
    replicas = seq_count // expert_count
    seq_place = lax.axis_index("seq")
    stacked = jnp.stack(
        (
            query_rows.reshape(tok_local, head_count, group_width),
            key_rows.reshape(tok_local, head_count, group_width),
            value_rows.reshape(tok_local, head_count, group_width),
        ),
        2,
    )
    by_head = lax.all_to_all(stacked, "head", split_axis=1, concat_axis=0, tiled=True)
    query_head = by_head[:, 0, 0]
    key_head = by_head[:, 0, 1]
    value_head = by_head[:, 0, 2]
    joined_head = by_head[:, 0, 1:].reshape(stretch_len, 2 * group_width)
    pieces = [joined_head]
    for distance in range(1, span_count):
        pieces.append(passed_along(joined_head, "seq", distance))
    joined_window = jnp.concatenate(pieces[::-1], 0)
    key_window = joined_window[:, :group_width]
    value_window = joined_window[:, group_width:]
    front_rows = (span_count - 1) * stretch_len
    all_segments = lax.all_gather(segment_ids, "seq", axis=0, tiled=True)
    segment_window = lax.dynamic_slice_in_dim(
        jnp.concatenate((jnp.zeros((front_rows,), jnp.int32), all_segments), 0),
        seq_place * stretch_len,
        span_count * stretch_len,
        0,
    )
    key_total = span_count * stretch_len
    query_place = seq_place * stretch_len + jnp.arange(stretch_len, dtype=jnp.int32)
    key_place = (seq_place - span_count + 1) * stretch_len + jnp.arange(key_total, dtype=jnp.int32)
    allowed = (
        (segment_window[None, :] == segment_ids[:, None])
        & (key_place[None, :] <= query_place[:, None])
        & (key_place[None, :] >= 0)
    )
    queries = query_head.reshape(stretch_len, heads_here, HDIM)
    keys_all = key_window.reshape(key_total, heads_here, HDIM)
    values_all = value_window.reshape(key_total, heads_here, HDIM)
    masked = score_piece(queries, keys_all, allowed)
    row_max = jnp.max(masked, -1, keepdims=True)
    weights = jnp.where(allowed[None], jnp.exp(masked - row_max), 0.0)
    totals = jnp.sum(weights, -1)
    mixture = mix_piece(weights.astype(jnp.bfloat16), values_all)
    attention = (
        (mixture / jnp.transpose(totals)[:, :, None])
        .astype(jnp.bfloat16)
        .reshape(stretch_len, group_width)
    )
    attended_sum = lax.psum_scatter(
        jnp.dot(attention, out_weight, preferred_element_type=jnp.float32).astype(jnp.bfloat16),
        "head",
        scatter_dimension=0,
        tiled=True,
    ).astype(jnp.float32)
    middle = (residual_in.astype(jnp.float32) + residual_scale * attended_sum).astype(jnp.bfloat16)
    middle_wide = middle.astype(jnp.float32)
    mean_square = jnp.mean(middle_wide * middle_wide, -1, keepdims=True)
    normed = (middle_wide * lax.rsqrt(mean_square + norm_epsilon) * norm_gain).astype(jnp.bfloat16)
    route_count = expert_ids.shape[1]
    logits = jnp.dot(normed, router_weight, preferred_element_type=jnp.float32)
    route_hot = expert_ids[:, :, None] == jnp.arange(expert_count, dtype=jnp.int32)[None, None, :]
    chosen = jnp.sum(jnp.where(route_hot, logits[:, None, :], 0.0), -1)
    first_weight = 1.0 / (1.0 + jnp.exp(chosen[:, 1] - chosen[:, 0]))
    second_weight = 1.0 / (1.0 + jnp.exp(chosen[:, 0] - chosen[:, 1]))
    flat_hot = route_hot.reshape(tok_local * route_count, expert_count).astype(jnp.int32)
    before_count = jnp.cumsum(flat_hot, 0) - flat_hot
    route_rank = jnp.sum(before_count * flat_hot, -1)
    slot_ids = (expert_ids.reshape(-1) * CAP + route_rank).reshape(tok_local, route_count)
    slot_total = expert_count * CAP
    dispatch = jnp.any(
        slot_ids[None, :, :] == jnp.arange(slot_total, dtype=jnp.int32)[:, None, None], -1
    ).astype(jnp.bfloat16)
    packed = (
        jnp.dot(dispatch, normed, preferred_element_type=jnp.float32)
        .astype(jnp.bfloat16)
        .reshape(expert_count, CAP, D)
    )
    outgoing = jnp.broadcast_to(packed[:, None], (expert_count, replicas, CAP, D)).reshape(
        seq_count, CAP, D
    )
    chunk_edges = (0, (CAP + 1) // 2, CAP)
    returned_parts = []
    for chunk_start, chunk_end in zip(chunk_edges[:-1], chunk_edges[1:]):
        slot_count = chunk_end - chunk_start
        arrived = lax.all_to_all(
            outgoing[:, chunk_start:chunk_end], "seq", split_axis=0, concat_axis=0, tiled=True
        )
        flat_rows = arrived.reshape(seq_count * slot_count, D)
        group_rows = lax.all_gather(flat_rows, "head", axis=0, tiled=True)
        gate_act = jnp.dot(group_rows, gate_weight, preferred_element_type=jnp.float32)
        up_act = jnp.dot(group_rows, up_weight, preferred_element_type=jnp.float32)
        hidden = (jax.nn.silu(gate_act) * up_act).astype(jnp.bfloat16)
        partial_out = lax.dot_general(
            hidden, down_weight, (((1,), (1,)), ((), ())), preferred_element_type=jnp.float32
        ).astype(jnp.bfloat16)
        shard_out = lax.psum_scatter(partial_out, "head", scatter_dimension=0, tiled=True)
        returned_parts.append(
            lax.all_to_all(
                shard_out.reshape(seq_count, slot_count, D),
                "seq",
                split_axis=0,
                concat_axis=0,
                tiled=True,
            )
        )
    returned = jnp.concatenate(returned_parts, 1)
    expert_out = jnp.sum(
        returned.reshape(expert_count, replicas, CAP, D).astype(jnp.float32), 1
    ).reshape(slot_total, D)
    first_rows = expert_out[slot_ids[:, 0]]
    second_rows = expert_out[slot_ids[:, 1]]
    moe_sum = first_weight[:, None] * first_rows + second_weight[:, None] * second_rows
    residual_out = (middle_wide + residual_scale * moe_sum).astype(jnp.bfloat16)
    return (residual_out, key_head, value_head)


def solution(mesh):
    return jax.shard_map(
        per_device,
        mesh=mesh,
        in_specs=(
            P(("seq", "head"), None),
            P(("seq", "head"), None),
            P(("seq", "head"), None),
            P(("seq", "head"), None),
            P(),
            P(),
            P("seq"),
            P(("seq", "head"), None),
            P(None, ("seq", "head")),
            P(None, ("seq", "head")),
            P(None, ("seq", "head")),
            P("head", None),
        ),
        out_specs=(P(("seq", "head"), None), P("seq", "head"), P("seq", "head")),
        check_vma=False,
    )
```

```python
import math

import jax
import jax.numpy as jnp
from jax import lax
from jax.sharding import PartitionSpec as P

D = 2304
HDIM = 64
LEVELS = 4
CAP = 9


residual_scale = 1.4 / math.sqrt(40.0)
norm_epsilon = 1e-05


def passed_along(value, axis, by):
    length = lax.axis_size(axis)
    pairs = [(i, i + by) for i in range(length) if 0 <= i + by < length]
    return lax.ppermute(value, axis, pairs)


def score_piece(queries, key_piece, piece_allowed):
    raw_scores = jnp.einsum(
        "qhd,khd->hqk", queries, key_piece, preferred_element_type=jnp.float32
    ) * queries.shape[2] ** (-0.5)
    return jnp.where(piece_allowed[None], raw_scores, -jnp.inf)


def mix_piece(rounded_piece, value_piece):
    return jnp.einsum(
        "hqk,khd->qhd", rounded_piece, value_piece, preferred_element_type=jnp.float32
    )


def per_device(
    query_rows,
    key_rows,
    value_rows,
    residual_in,
    norm_gain,
    router_weight,
    segment_ids,
    expert_ids,
    gate_weight,
    up_weight,
    down_weight,
    out_weight,
):
    head_count = lax.axis_size("head")
    seq_count = lax.axis_size("seq")
    tok_local = query_rows.shape[0]
    group_width = query_rows.shape[1] // head_count
    heads_here = group_width // HDIM
    stretch_len = tok_local * head_count
    span_count = min(2**LEVELS * 32 // tok_local, seq_count)
    expert_count = router_weight.shape[1]
    replicas = seq_count // expert_count
    seq_place = lax.axis_index("seq")
    stacked = jnp.stack(
        (
            query_rows.reshape(tok_local, head_count, group_width),
            key_rows.reshape(tok_local, head_count, group_width),
            value_rows.reshape(tok_local, head_count, group_width),
        ),
        2,
    )
    by_head = lax.all_to_all(stacked, "head", split_axis=1, concat_axis=0, tiled=True)
    query_head = by_head[:, 0, 0]
    key_head = by_head[:, 0, 1]
    value_head = by_head[:, 0, 2]
    joined_head = by_head[:, 0, 1:].reshape(stretch_len, 2 * group_width)
    all_segments = lax.all_gather(segment_ids, "seq", axis=0, tiled=True)
    if span_count == seq_count:
        joined_window = lax.all_gather(joined_head, "seq", axis=0, tiled=True)
        segment_window = all_segments
        window_first = 0
    else:
        pieces = [joined_head]
        for distance in range(1, span_count):
            pieces.append(passed_along(joined_head, "seq", distance))
        joined_window = jnp.concatenate(pieces[::-1], 0)
        front_rows = (span_count - 1) * stretch_len
        segment_window = lax.dynamic_slice_in_dim(
            jnp.concatenate((jnp.zeros((front_rows,), jnp.int32), all_segments), 0),
            seq_place * stretch_len,
            span_count * stretch_len,
            0,
        )
        window_first = (seq_place - span_count + 1) * stretch_len
    key_window = joined_window[:, :group_width]
    value_window = joined_window[:, group_width:]
    key_total = span_count * stretch_len
    query_place = seq_place * stretch_len + jnp.arange(stretch_len, dtype=jnp.int32)
    key_place = window_first + jnp.arange(key_total, dtype=jnp.int32)
    allowed = (
        (segment_window[None, :] == segment_ids[:, None])
        & (key_place[None, :] <= query_place[:, None])
        & (key_place[None, :] >= 0)
    )
    queries = query_head.reshape(stretch_len, heads_here, HDIM)
    keys_all = key_window.reshape(key_total, heads_here, HDIM)
    values_all = value_window.reshape(key_total, heads_here, HDIM)
    masked = score_piece(queries, keys_all, allowed)
    row_max = jnp.max(masked, -1, keepdims=True)
    weights = jnp.where(allowed[None], jnp.exp(masked - row_max), 0.0)
    totals = jnp.sum(weights, -1)
    mixture = mix_piece(weights.astype(jnp.bfloat16), values_all)
    attention = (
        (mixture / jnp.transpose(totals)[:, :, None])
        .astype(jnp.bfloat16)
        .reshape(stretch_len, group_width)
    )
    attended_sum = lax.psum_scatter(
        jnp.dot(attention, out_weight, preferred_element_type=jnp.float32).astype(jnp.bfloat16),
        "head",
        scatter_dimension=0,
        tiled=True,
    ).astype(jnp.float32)
    middle = (residual_in.astype(jnp.float32) + residual_scale * attended_sum).astype(jnp.bfloat16)
    middle_wide = middle.astype(jnp.float32)
    mean_square = jnp.mean(middle_wide * middle_wide, -1, keepdims=True)
    normed = (middle_wide * lax.rsqrt(mean_square + norm_epsilon) * norm_gain).astype(jnp.bfloat16)
    route_count = expert_ids.shape[1]
    logits = jnp.dot(normed, router_weight, preferred_element_type=jnp.float32)
    route_hot = expert_ids[:, :, None] == jnp.arange(expert_count, dtype=jnp.int32)[None, None, :]
    chosen = jnp.sum(jnp.where(route_hot, logits[:, None, :], 0.0), -1)
    first_weight = 1.0 / (1.0 + jnp.exp(chosen[:, 1] - chosen[:, 0]))
    second_weight = 1.0 / (1.0 + jnp.exp(chosen[:, 0] - chosen[:, 1]))
    flat_hot = route_hot.reshape(tok_local * route_count, expert_count).astype(jnp.int32)
    before_count = jnp.cumsum(flat_hot, 0) - flat_hot
    route_rank = jnp.sum(before_count * flat_hot, -1)
    slot_ids = (expert_ids.reshape(-1) * CAP + route_rank).reshape(tok_local, route_count)
    slot_total = expert_count * CAP
    dispatch = jnp.any(
        slot_ids[None, :, :] == jnp.arange(slot_total, dtype=jnp.int32)[:, None, None], -1
    ).astype(jnp.bfloat16)
    packed = (
        jnp.dot(dispatch, normed, preferred_element_type=jnp.float32)
        .astype(jnp.bfloat16)
        .reshape(expert_count, CAP, D)
    )
    outgoing = jnp.broadcast_to(packed[:, None], (expert_count, replicas, CAP, D)).reshape(
        seq_count, CAP, D
    )
    arrived = lax.all_to_all(outgoing, "seq", split_axis=0, concat_axis=0, tiled=True)
    slot_count = arrived.shape[1]
    flat_rows = arrived.reshape(seq_count * slot_count, D)
    group_rows = lax.all_gather(flat_rows, "head", axis=0, tiled=True)
    gate_act = jnp.dot(group_rows, gate_weight, preferred_element_type=jnp.float32)
    up_act = jnp.dot(group_rows, up_weight, preferred_element_type=jnp.float32)
    hidden = (jax.nn.silu(gate_act) * up_act).astype(jnp.bfloat16)
    partial_out = lax.dot_general(
        hidden, down_weight, (((1,), (1,)), ((), ())), preferred_element_type=jnp.float32
    ).astype(jnp.bfloat16)
    shard_out = lax.psum_scatter(partial_out, "head", scatter_dimension=0, tiled=True)
    returned = lax.all_to_all(
        shard_out.reshape(seq_count, slot_count, D), "seq", split_axis=0, concat_axis=0, tiled=True
    )
    expert_out = jnp.sum(
        returned.reshape(expert_count, replicas, CAP, D).astype(jnp.float32), 1
    ).reshape(slot_total, D)
    first_rows = expert_out[slot_ids[:, 0]]
    second_rows = expert_out[slot_ids[:, 1]]
    moe_sum = first_weight[:, None] * first_rows + second_weight[:, None] * second_rows
    residual_out = (middle_wide + residual_scale * moe_sum).astype(jnp.bfloat16)
    return (residual_out, key_head, value_head)


def solution(mesh):
    return jax.shard_map(
        per_device,
        mesh=mesh,
        in_specs=(
            P(("seq", "head"), None),
            P(("seq", "head"), None),
            P(("seq", "head"), None),
            P(("seq", "head"), None),
            P(),
            P(),
            P("seq"),
            P(("seq", "head"), None),
            P(None, ("seq", "head")),
            P(None, ("seq", "head")),
            P(None, ("seq", "head")),
            P("head", None),
        ),
        out_specs=(P(("seq", "head"), None), P("seq", "head"), P("seq", "head")),
        check_vma=False,
    )
```

```python
import math

import jax
import jax.numpy as jnp
from jax import lax
from jax.sharding import PartitionSpec as P

D = 2304
HDIM = 64
LEVELS = 4
CAP = 9


residual_scale = 1.4 / math.sqrt(40.0)
norm_epsilon = 1e-05


def passed_along(value, axis, by):
    length = lax.axis_size(axis)
    pairs = [(i, i + by) for i in range(length) if 0 <= i + by < length]
    return lax.ppermute(value, axis, pairs)


def score_piece(queries, key_piece, piece_allowed):
    raw_scores = jnp.einsum(
        "qhd,khd->hqk", queries, key_piece, preferred_element_type=jnp.float32
    ) * queries.shape[2] ** (-0.5)
    return jnp.where(piece_allowed[None], raw_scores, -jnp.inf)


def mix_piece(rounded_piece, value_piece):
    return jnp.einsum(
        "hqk,khd->qhd", rounded_piece, value_piece, preferred_element_type=jnp.float32
    )


def per_device(
    query_rows,
    key_rows,
    value_rows,
    residual_in,
    norm_gain,
    router_weight,
    segment_ids,
    expert_ids,
    gate_weight,
    up_weight,
    down_weight,
    out_weight,
):
    head_count = lax.axis_size("head")
    seq_count = lax.axis_size("seq")
    tok_local = query_rows.shape[0]
    group_width = query_rows.shape[1] // head_count
    heads_here = group_width // HDIM
    stretch_len = tok_local * head_count
    span_count = min(2**LEVELS * 32 // tok_local, seq_count)
    expert_count = router_weight.shape[1]
    replicas = seq_count // expert_count
    seq_place = lax.axis_index("seq")
    joined_stack = jnp.stack(
        (
            key_rows.reshape(tok_local, head_count, group_width),
            value_rows.reshape(tok_local, head_count, group_width),
        ),
        2,
    )
    joined_by_head = lax.all_to_all(joined_stack, "head", split_axis=1, concat_axis=0, tiled=True)
    key_head = joined_by_head[:, 0, 0]
    value_head = joined_by_head[:, 0, 1]
    joined_head = joined_by_head.reshape(stretch_len, 2 * group_width)
    query_head = lax.all_to_all(
        query_rows.reshape(tok_local, head_count, group_width),
        "head",
        split_axis=1,
        concat_axis=0,
        tiled=True,
    ).reshape(stretch_len, group_width)
    all_segments = lax.all_gather(segment_ids, "seq", axis=0, tiled=True)
    if span_count == seq_count:
        joined_window = lax.all_gather(joined_head, "seq", axis=0, tiled=True)
        segment_window = all_segments
        window_first = 0
    else:
        pieces = [joined_head]
        for distance in range(1, span_count):
            pieces.append(passed_along(joined_head, "seq", distance))
        joined_window = jnp.concatenate(pieces[::-1], 0)
        front_rows = (span_count - 1) * stretch_len
        segment_window = lax.dynamic_slice_in_dim(
            jnp.concatenate((jnp.zeros((front_rows,), jnp.int32), all_segments), 0),
            seq_place * stretch_len,
            span_count * stretch_len,
            0,
        )
        window_first = (seq_place - span_count + 1) * stretch_len
    key_window = joined_window[:, :group_width]
    value_window = joined_window[:, group_width:]
    key_total = span_count * stretch_len
    query_place = seq_place * stretch_len + jnp.arange(stretch_len, dtype=jnp.int32)
    key_place = window_first + jnp.arange(key_total, dtype=jnp.int32)
    allowed = (
        (segment_window[None, :] == segment_ids[:, None])
        & (key_place[None, :] <= query_place[:, None])
        & (key_place[None, :] >= 0)
    )
    queries = query_head.reshape(stretch_len, heads_here, HDIM)
    keys_all = key_window.reshape(key_total, heads_here, HDIM)
    values_all = value_window.reshape(key_total, heads_here, HDIM)
    masked = score_piece(queries, keys_all, allowed)
    row_max = jnp.max(masked, -1, keepdims=True)
    weights = jnp.where(allowed[None], jnp.exp(masked - row_max), 0.0)
    totals = jnp.sum(weights, -1)
    mixture = mix_piece(weights.astype(jnp.bfloat16), values_all)
    attention = (
        (mixture / jnp.transpose(totals)[:, :, None])
        .astype(jnp.bfloat16)
        .reshape(stretch_len, group_width)
    )
    attended_sum = lax.psum_scatter(
        jnp.dot(attention, out_weight, preferred_element_type=jnp.float32).astype(jnp.bfloat16),
        "head",
        scatter_dimension=0,
        tiled=True,
    ).astype(jnp.float32)
    middle = (residual_in.astype(jnp.float32) + residual_scale * attended_sum).astype(jnp.bfloat16)
    middle_wide = middle.astype(jnp.float32)
    mean_square = jnp.mean(middle_wide * middle_wide, -1, keepdims=True)
    normed = (middle_wide * lax.rsqrt(mean_square + norm_epsilon) * norm_gain).astype(jnp.bfloat16)
    route_count = expert_ids.shape[1]
    logits = jnp.dot(normed, router_weight, preferred_element_type=jnp.float32)
    route_hot = expert_ids[:, :, None] == jnp.arange(expert_count, dtype=jnp.int32)[None, None, :]
    chosen = jnp.sum(jnp.where(route_hot, logits[:, None, :], 0.0), -1)
    first_weight = 1.0 / (1.0 + jnp.exp(chosen[:, 1] - chosen[:, 0]))
    second_weight = 1.0 / (1.0 + jnp.exp(chosen[:, 0] - chosen[:, 1]))
    flat_hot = route_hot.reshape(tok_local * route_count, expert_count).astype(jnp.int32)
    before_count = jnp.cumsum(flat_hot, 0) - flat_hot
    route_rank = jnp.sum(before_count * flat_hot, -1)
    slot_ids = (expert_ids.reshape(-1) * CAP + route_rank).reshape(tok_local, route_count)
    slot_total = expert_count * CAP
    dispatch = jnp.any(
        slot_ids[None, :, :] == jnp.arange(slot_total, dtype=jnp.int32)[:, None, None], -1
    ).astype(jnp.bfloat16)
    packed = (
        jnp.dot(dispatch, normed, preferred_element_type=jnp.float32)
        .astype(jnp.bfloat16)
        .reshape(expert_count, CAP, D)
    )
    outgoing = jnp.broadcast_to(packed[:, None], (expert_count, replicas, CAP, D)).reshape(
        seq_count, CAP, D
    )
    arrived = lax.all_to_all(outgoing, "seq", split_axis=0, concat_axis=0, tiled=True)
    slot_count = arrived.shape[1]
    flat_rows = arrived.reshape(seq_count * slot_count, D)
    group_rows = lax.all_gather(flat_rows, "head", axis=0, tiled=True)
    gate_act = jnp.dot(group_rows, gate_weight, preferred_element_type=jnp.float32)
    up_act = jnp.dot(group_rows, up_weight, preferred_element_type=jnp.float32)
    hidden = (jax.nn.silu(gate_act) * up_act).astype(jnp.bfloat16)
    partial_out = lax.dot_general(
        hidden, down_weight, (((1,), (1,)), ((), ())), preferred_element_type=jnp.float32
    ).astype(jnp.bfloat16)
    shard_out = lax.psum_scatter(partial_out, "head", scatter_dimension=0, tiled=True)
    returned = lax.all_to_all(
        shard_out.reshape(seq_count, slot_count, D), "seq", split_axis=0, concat_axis=0, tiled=True
    )
    by_slot = jnp.swapaxes(returned.reshape(expert_count, replicas, CAP, D), 1, 2).reshape(
        slot_total, replicas, D
    )
    slot_range = jnp.arange(slot_total, dtype=jnp.int32)[None, :]
    first_hot = (slot_ids[:, 0:1] == slot_range).astype(jnp.bfloat16)
    second_hot = (slot_ids[:, 1:2] == slot_range).astype(jnp.bfloat16)
    first_rows = jnp.sum(
        jnp.einsum("ts,srd->trd", first_hot, by_slot, preferred_element_type=jnp.float32), 1
    )
    second_rows = jnp.sum(
        jnp.einsum("ts,srd->trd", second_hot, by_slot, preferred_element_type=jnp.float32), 1
    )
    moe_sum = first_weight[:, None] * first_rows + second_weight[:, None] * second_rows
    residual_out = (middle_wide + residual_scale * moe_sum).astype(jnp.bfloat16)
    return (residual_out, key_head, value_head)


def solution(mesh):
    return jax.shard_map(
        per_device,
        mesh=mesh,
        in_specs=(
            P(("seq", "head"), None),
            P(("seq", "head"), None),
            P(("seq", "head"), None),
            P(("seq", "head"), None),
            P(),
            P(),
            P("seq"),
            P(("seq", "head"), None),
            P(None, ("seq", "head")),
            P(None, ("seq", "head")),
            P(None, ("seq", "head")),
            P("head", None),
        ),
        out_specs=(P(("seq", "head"), None), P("seq", "head"), P("seq", "head")),
        check_vma=False,
    )
```

```python
import math

import jax
import jax.numpy as jnp
from jax import lax
from jax.sharding import PartitionSpec as P

D = 2304
HDIM = 64
LEVELS = 4
CAP = 9


residual_scale = 1.4 / math.sqrt(40.0)
norm_epsilon = 1e-05


def passed_along(value, axis, by):
    length = lax.axis_size(axis)
    pairs = [(i, i + by) for i in range(length) if 0 <= i + by < length]
    return lax.ppermute(value, axis, pairs)


def score_piece(queries, key_piece, piece_allowed):
    raw_scores = jnp.einsum(
        "qhd,khd->hqk", queries, key_piece, preferred_element_type=jnp.float32
    ) * queries.shape[2] ** (-0.5)
    return jnp.where(piece_allowed[None], raw_scores, -jnp.inf)


def mix_piece(rounded_piece, value_piece):
    return jnp.einsum(
        "hqk,khd->qhd", rounded_piece, value_piece, preferred_element_type=jnp.float32
    )


def per_device(
    query_rows,
    key_rows,
    value_rows,
    residual_in,
    norm_gain,
    router_weight,
    segment_ids,
    expert_ids,
    gate_weight,
    up_weight,
    down_weight,
    out_weight,
):
    head_count = lax.axis_size("head")
    seq_count = lax.axis_size("seq")
    tok_local = query_rows.shape[0]
    group_width = query_rows.shape[1] // head_count
    heads_here = group_width // HDIM
    stretch_len = tok_local * head_count
    span_count = min(2**LEVELS * 32 // tok_local, seq_count)
    expert_count = router_weight.shape[1]
    replicas = seq_count // expert_count
    seq_place = lax.axis_index("seq")
    joined_stack = jnp.stack(
        (
            key_rows.reshape(tok_local, head_count, group_width),
            value_rows.reshape(tok_local, head_count, group_width),
        ),
        2,
    )
    joined_by_head = lax.all_to_all(joined_stack, "head", split_axis=1, concat_axis=0, tiled=True)
    key_head = joined_by_head[:, 0, 0]
    value_head = joined_by_head[:, 0, 1]
    joined_head = joined_by_head.reshape(stretch_len, 2 * group_width)
    query_head = lax.all_to_all(
        query_rows.reshape(tok_local, head_count, group_width),
        "head",
        split_axis=1,
        concat_axis=0,
        tiled=True,
    ).reshape(stretch_len, group_width)
    all_segments = lax.all_gather(segment_ids, "seq", axis=0, tiled=True)
    if span_count == seq_count:
        joined_window = lax.all_gather(joined_head, "seq", axis=0, tiled=True)
        segment_window = all_segments
        window_first = 0
    else:
        pieces = [joined_head]
        for distance in range(1, span_count):
            pieces.append(passed_along(joined_head, "seq", distance))
        joined_window = jnp.concatenate(pieces[::-1], 0)
        front_rows = (span_count - 1) * stretch_len
        segment_window = lax.dynamic_slice_in_dim(
            jnp.concatenate((jnp.zeros((front_rows,), jnp.int32), all_segments), 0),
            seq_place * stretch_len,
            span_count * stretch_len,
            0,
        )
        window_first = (seq_place - span_count + 1) * stretch_len
    key_window = joined_window[:, :group_width]
    value_window = joined_window[:, group_width:]
    key_total = span_count * stretch_len
    query_place = seq_place * stretch_len + jnp.arange(stretch_len, dtype=jnp.int32)
    key_place = window_first + jnp.arange(key_total, dtype=jnp.int32)
    allowed = (
        (segment_window[None, :] == segment_ids[:, None])
        & (key_place[None, :] <= query_place[:, None])
        & (key_place[None, :] >= 0)
    )
    queries = query_head.reshape(stretch_len, heads_here, HDIM)
    keys_all = key_window.reshape(key_total, heads_here, HDIM)
    values_all = value_window.reshape(key_total, heads_here, HDIM)
    masked = score_piece(queries, keys_all, allowed)
    row_max = jnp.max(masked, -1, keepdims=True)
    weights = jnp.where(allowed[None], jnp.exp(masked - row_max), 0.0)
    totals = jnp.sum(weights, -1)
    mixture = mix_piece(weights.astype(jnp.bfloat16), values_all)
    attention = (
        (mixture / jnp.transpose(totals)[:, :, None])
        .astype(jnp.bfloat16)
        .reshape(stretch_len, group_width)
    )
    attended_sum = lax.psum_scatter(
        jnp.dot(attention, out_weight, preferred_element_type=jnp.float32).astype(jnp.bfloat16),
        "head",
        scatter_dimension=0,
        tiled=True,
    ).astype(jnp.float32)
    middle = (residual_in.astype(jnp.float32) + residual_scale * attended_sum).astype(jnp.bfloat16)
    middle_wide = middle.astype(jnp.float32)
    mean_square = jnp.mean(middle_wide * middle_wide, -1, keepdims=True)
    normed = (middle_wide * lax.rsqrt(mean_square + norm_epsilon) * norm_gain).astype(jnp.bfloat16)
    route_count = expert_ids.shape[1]
    logits = jnp.dot(normed, router_weight, preferred_element_type=jnp.float32)
    route_hot = expert_ids[:, :, None] == jnp.arange(expert_count, dtype=jnp.int32)[None, None, :]
    chosen = jnp.sum(jnp.where(route_hot, logits[:, None, :], 0.0), -1)
    first_weight = 1.0 / (1.0 + jnp.exp(chosen[:, 1] - chosen[:, 0]))
    second_weight = 1.0 / (1.0 + jnp.exp(chosen[:, 0] - chosen[:, 1]))
    flat_hot = route_hot.reshape(tok_local * route_count, expert_count).astype(jnp.int32)
    before_count = jnp.cumsum(flat_hot, 0) - flat_hot
    route_rank = jnp.sum(before_count * flat_hot, -1)
    slot_ids = (expert_ids.reshape(-1) * CAP + route_rank).reshape(tok_local, route_count)
    slot_total = expert_count * CAP
    normed_group = lax.all_gather(normed, "head", axis=0, tiled=True)
    ids_group = lax.all_gather(expert_ids, "head", axis=0, tiled=True).reshape(
        head_count, tok_local * route_count
    )
    group_hot = (
        ids_group[:, :, None] == jnp.arange(expert_count, dtype=jnp.int32)[None, None, :]
    ).astype(jnp.int32)
    group_rank = jnp.sum((jnp.cumsum(group_hot, 1) - group_hot) * group_hot, -1)
    source_place = jnp.arange(head_count, dtype=jnp.int32)[:, None]
    row_ids = ((ids_group * head_count + source_place) * CAP + group_rank).reshape(
        head_count * tok_local, route_count
    )
    row_total = expert_count * head_count * CAP
    group_dispatch = jnp.any(
        row_ids[None, :, :] == jnp.arange(row_total, dtype=jnp.int32)[:, None, None], -1
    ).astype(jnp.bfloat16)
    packed = (
        jnp.dot(group_dispatch, normed_group, preferred_element_type=jnp.float32)
        .astype(jnp.bfloat16)
        .reshape(expert_count, head_count * CAP, D)
    )
    outgoing = jnp.broadcast_to(
        packed[:, None], (expert_count, replicas, head_count * CAP, D)
    ).reshape(seq_count, head_count * CAP, D)
    arrived = lax.all_to_all(outgoing, "seq", split_axis=0, concat_axis=0, tiled=True)
    slot_count = CAP
    group_rows = jnp.swapaxes(arrived.reshape(seq_count, head_count, CAP, D), 0, 1).reshape(
        head_count * seq_count * CAP, D
    )
    gate_act = jnp.dot(group_rows, gate_weight, preferred_element_type=jnp.float32)
    up_act = jnp.dot(group_rows, up_weight, preferred_element_type=jnp.float32)
    hidden = (jax.nn.silu(gate_act) * up_act).astype(jnp.bfloat16)
    partial_out = lax.dot_general(
        hidden, down_weight, (((1,), (1,)), ((), ())), preferred_element_type=jnp.float32
    ).astype(jnp.bfloat16)
    shard_out = lax.psum_scatter(partial_out, "head", scatter_dimension=0, tiled=True)
    returned = lax.all_to_all(
        shard_out.reshape(seq_count, slot_count, D), "seq", split_axis=0, concat_axis=0, tiled=True
    )
    by_slot = jnp.swapaxes(returned.reshape(expert_count, replicas, CAP, D), 1, 2).reshape(
        slot_total, replicas, D
    )
    slot_range = jnp.arange(slot_total, dtype=jnp.int32)[None, :]
    first_hot = (slot_ids[:, 0:1] == slot_range).astype(jnp.bfloat16)
    second_hot = (slot_ids[:, 1:2] == slot_range).astype(jnp.bfloat16)
    first_rows = jnp.sum(
        jnp.einsum("ts,srd->trd", first_hot, by_slot, preferred_element_type=jnp.float32), 1
    )
    second_rows = jnp.sum(
        jnp.einsum("ts,srd->trd", second_hot, by_slot, preferred_element_type=jnp.float32), 1
    )
    moe_sum = first_weight[:, None] * first_rows + second_weight[:, None] * second_rows
    residual_out = (middle_wide + residual_scale * moe_sum).astype(jnp.bfloat16)
    return (residual_out, key_head, value_head)


def solution(mesh):
    return jax.shard_map(
        per_device,
        mesh=mesh,
        in_specs=(
            P(("seq", "head"), None),
            P(("seq", "head"), None),
            P(("seq", "head"), None),
            P(("seq", "head"), None),
            P(),
            P(),
            P("seq"),
            P(("seq", "head"), None),
            P(None, ("seq", "head")),
            P(None, ("seq", "head")),
            P(None, ("seq", "head")),
            P("head", None),
        ),
        out_specs=(P(("seq", "head"), None), P("seq", "head"), P("seq", "head")),
        check_vma=False,
    )
```

```python
import math

import jax
import jax.numpy as jnp
from jax import lax
from jax.sharding import PartitionSpec as P

D = 2304
HDIM = 64
LEVELS = 4
CAP = 9


residual_scale = 1.4 / math.sqrt(40.0)
norm_epsilon = 1e-05


def passed_along(value, axis, by):
    length = lax.axis_size(axis)
    pairs = [(i, i + by) for i in range(length) if 0 <= i + by < length]
    return lax.ppermute(value, axis, pairs)


def score_piece(queries, key_piece, piece_allowed):
    raw_scores = jnp.einsum(
        "qhd,khd->hqk", queries, key_piece, preferred_element_type=jnp.float32
    ) * queries.shape[2] ** (-0.5)
    return jnp.where(piece_allowed[None], raw_scores, -jnp.inf)


def mix_piece(rounded_piece, value_piece):
    return jnp.einsum(
        "hqk,khd->qhd", rounded_piece, value_piece, preferred_element_type=jnp.float32
    )


def per_device(
    query_rows,
    key_rows,
    value_rows,
    residual_in,
    norm_gain,
    router_weight,
    segment_ids,
    expert_ids,
    gate_weight,
    up_weight,
    down_weight,
    out_weight,
):
    head_count = lax.axis_size("head")
    seq_count = lax.axis_size("seq")
    tok_local = query_rows.shape[0]
    group_width = query_rows.shape[1] // head_count
    heads_here = group_width // HDIM
    stretch_len = tok_local * head_count
    span_count = min(2**LEVELS * 32 // tok_local, seq_count)
    expert_count = router_weight.shape[1]
    replicas = seq_count // expert_count
    seq_place = lax.axis_index("seq")
    joined_rows = jnp.concatenate(
        (
            key_rows.reshape(tok_local, head_count, group_width),
            value_rows.reshape(tok_local, head_count, group_width),
        ),
        2,
    )
    joined_head = lax.all_to_all(
        joined_rows, "head", split_axis=1, concat_axis=0, tiled=True
    ).reshape(stretch_len, 2 * group_width)
    key_head = joined_head[:, :group_width]
    value_head = joined_head[:, group_width:]
    query_head = lax.all_to_all(
        query_rows.reshape(tok_local, head_count, group_width),
        "head",
        split_axis=1,
        concat_axis=0,
        tiled=True,
    ).reshape(stretch_len, group_width)
    all_segments = lax.all_gather(segment_ids, "seq", axis=0, tiled=True)
    if span_count == seq_count:
        joined_window = lax.all_gather(joined_head, "seq", axis=0, tiled=True)
        segment_window = all_segments
        window_first = 0
    else:
        pieces = [joined_head]
        for distance in range(1, span_count):
            pieces.append(passed_along(joined_head, "seq", distance))
        joined_window = jnp.concatenate(pieces[::-1], 0)
        front_rows = (span_count - 1) * stretch_len
        segment_window = lax.dynamic_slice_in_dim(
            jnp.concatenate((jnp.zeros((front_rows,), jnp.int32), all_segments), 0),
            seq_place * stretch_len,
            span_count * stretch_len,
            0,
        )
        window_first = (seq_place - span_count + 1) * stretch_len
    key_window = joined_window[:, :group_width]
    value_window = joined_window[:, group_width:]
    key_total = span_count * stretch_len
    query_place = seq_place * stretch_len + jnp.arange(stretch_len, dtype=jnp.int32)
    key_place = window_first + jnp.arange(key_total, dtype=jnp.int32)
    allowed = (
        (segment_window[None, :] == segment_ids[:, None])
        & (key_place[None, :] <= query_place[:, None])
        & (key_place[None, :] >= 0)
    )
    queries = query_head.reshape(stretch_len, heads_here, HDIM)
    keys_all = key_window.reshape(key_total, heads_here, HDIM)
    values_all = value_window.reshape(key_total, heads_here, HDIM)
    masked = score_piece(queries, keys_all, allowed)
    row_max = jnp.max(masked, -1, keepdims=True)
    weights = jnp.where(allowed[None], jnp.exp(masked - row_max), 0.0)
    totals = jnp.sum(weights, -1)
    mixture = mix_piece(weights.astype(jnp.bfloat16), values_all)
    attention = (
        (mixture / jnp.transpose(totals)[:, :, None])
        .astype(jnp.bfloat16)
        .reshape(stretch_len, group_width)
    )
    attended_sum = lax.psum_scatter(
        jnp.dot(attention, out_weight, preferred_element_type=jnp.float32).astype(jnp.bfloat16),
        "head",
        scatter_dimension=0,
        tiled=True,
    ).astype(jnp.float32)
    middle = (residual_in.astype(jnp.float32) + residual_scale * attended_sum).astype(jnp.bfloat16)
    middle_wide = middle.astype(jnp.float32)
    mean_square = jnp.mean(middle_wide * middle_wide, -1, keepdims=True)
    normed = (middle_wide * lax.rsqrt(mean_square + norm_epsilon) * norm_gain).astype(jnp.bfloat16)
    route_count = expert_ids.shape[1]
    logits = jnp.dot(normed, router_weight, preferred_element_type=jnp.float32)
    route_hot = expert_ids[:, :, None] == jnp.arange(expert_count, dtype=jnp.int32)[None, None, :]
    chosen = jnp.sum(jnp.where(route_hot, logits[:, None, :], 0.0), -1)
    first_weight = 1.0 / (1.0 + jnp.exp(chosen[:, 1] - chosen[:, 0]))
    second_weight = 1.0 / (1.0 + jnp.exp(chosen[:, 0] - chosen[:, 1]))
    flat_hot = route_hot.reshape(tok_local * route_count, expert_count).astype(jnp.int32)
    before_count = jnp.cumsum(flat_hot, 0) - flat_hot
    route_rank = jnp.sum(before_count * flat_hot, -1)
    slot_ids = (expert_ids.reshape(-1) * CAP + route_rank).reshape(tok_local, route_count)
    slot_total = expert_count * CAP
    dispatch = jnp.any(
        slot_ids[None, :, :] == jnp.arange(slot_total, dtype=jnp.int32)[:, None, None], -1
    ).astype(jnp.bfloat16)
    packed = (
        jnp.dot(dispatch, normed, preferred_element_type=jnp.float32)
        .astype(jnp.bfloat16)
        .reshape(expert_count, CAP, D)
    )
    outgoing = jnp.broadcast_to(packed[:, None], (expert_count, replicas, CAP, D)).reshape(
        seq_count, CAP, D
    )
    arrived = lax.all_to_all(outgoing, "seq", split_axis=0, concat_axis=0, tiled=True)
    slot_count = arrived.shape[1]
    flat_rows = arrived.reshape(seq_count * slot_count, D)
    group_rows = lax.all_gather(flat_rows, "head", axis=0, tiled=True).reshape(
        head_count, seq_count, slot_count, D
    )
    chunk_edges = (0, (slot_count + 1) // 2, slot_count)
    returned_parts = []
    for chunk_start, chunk_end in zip(chunk_edges[:-1], chunk_edges[1:]):
        chunk_slots = chunk_end - chunk_start
        chunk_rows = group_rows[:, :, chunk_start:chunk_end].reshape(
            head_count * seq_count * chunk_slots, D
        )
        gate_act = jnp.dot(chunk_rows, gate_weight, preferred_element_type=jnp.float32)
        up_act = jnp.dot(chunk_rows, up_weight, preferred_element_type=jnp.float32)
        hidden = (jax.nn.silu(gate_act) * up_act).astype(jnp.bfloat16)
        partial_out = lax.dot_general(
            hidden, down_weight, (((1,), (1,)), ((), ())), preferred_element_type=jnp.float32
        ).astype(jnp.bfloat16)
        shard_out = lax.psum_scatter(partial_out, "head", scatter_dimension=0, tiled=True)
        returned_parts.append(
            lax.all_to_all(
                shard_out.reshape(seq_count, chunk_slots, D),
                "seq",
                split_axis=0,
                concat_axis=0,
                tiled=True,
            )
        )
    returned = jnp.concatenate(returned_parts, 1)
    by_slot = jnp.swapaxes(returned.reshape(expert_count, replicas, CAP, D), 1, 2).reshape(
        slot_total, replicas, D
    )
    slot_range = jnp.arange(slot_total, dtype=jnp.int32)[None, :]
    first_hot = (slot_ids[:, 0:1] == slot_range).astype(jnp.bfloat16)
    second_hot = (slot_ids[:, 1:2] == slot_range).astype(jnp.bfloat16)
    first_rows = jnp.sum(
        jnp.einsum("ts,srd->trd", first_hot, by_slot, preferred_element_type=jnp.float32), 1
    )
    second_rows = jnp.sum(
        jnp.einsum("ts,srd->trd", second_hot, by_slot, preferred_element_type=jnp.float32), 1
    )
    moe_sum = first_weight[:, None] * first_rows + second_weight[:, None] * second_rows
    residual_out = (middle_wide + residual_scale * moe_sum).astype(jnp.bfloat16)
    return (residual_out, key_head, value_head)


def solution(mesh):
    return jax.shard_map(
        per_device,
        mesh=mesh,
        in_specs=(
            P(("seq", "head"), None),
            P(("seq", "head"), None),
            P(("seq", "head"), None),
            P(("seq", "head"), None),
            P(),
            P(),
            P("seq"),
            P(("seq", "head"), None),
            P(None, ("seq", "head")),
            P(None, ("seq", "head")),
            P(None, ("seq", "head")),
            P("head", None),
        ),
        out_specs=(P(("seq", "head"), None), P("seq", "head"), P("seq", "head")),
        check_vma=False,
    )
```

```python
import math

import jax
import jax.numpy as jnp
from jax import lax
from jax.sharding import PartitionSpec as P

D = 2304
HDIM = 64
LEVELS = 4
CAP = 9


residual_scale = 1.4 / math.sqrt(40.0)
norm_epsilon = 1e-05


def passed_along(value, axis, by):
    length = lax.axis_size(axis)
    pairs = [(i, i + by) for i in range(length) if 0 <= i + by < length]
    return lax.ppermute(value, axis, pairs)


def score_piece(queries, key_piece, piece_allowed):
    raw_scores = jnp.einsum(
        "qhd,khd->hqk", queries, key_piece, preferred_element_type=jnp.float32
    ) * queries.shape[2] ** (-0.5)
    return jnp.where(piece_allowed[None], raw_scores, -jnp.inf)


def mix_piece(rounded_piece, value_piece):
    return jnp.einsum(
        "hqk,khd->qhd", rounded_piece, value_piece, preferred_element_type=jnp.float32
    )


def per_device(
    query_rows,
    key_rows,
    value_rows,
    residual_in,
    norm_gain,
    router_weight,
    segment_ids,
    expert_ids,
    gate_weight,
    up_weight,
    down_weight,
    out_weight,
):
    head_count = lax.axis_size("head")
    seq_count = lax.axis_size("seq")
    tok_local = query_rows.shape[0]
    group_width = query_rows.shape[1] // head_count
    heads_here = group_width // HDIM
    stretch_len = tok_local * head_count
    span_count = min(2**LEVELS * 32 // tok_local, seq_count)
    expert_count = router_weight.shape[1]
    replicas = seq_count // expert_count
    seq_place = lax.axis_index("seq")
    joined_rows = jnp.concatenate(
        (
            key_rows.reshape(tok_local, head_count, group_width),
            value_rows.reshape(tok_local, head_count, group_width),
        ),
        2,
    )
    joined_head = lax.all_to_all(
        joined_rows, "head", split_axis=1, concat_axis=0, tiled=True
    ).reshape(stretch_len, 2 * group_width)
    key_head = joined_head[:, :group_width]
    value_head = joined_head[:, group_width:]
    query_head = lax.all_to_all(
        query_rows.reshape(tok_local, head_count, group_width),
        "head",
        split_axis=1,
        concat_axis=0,
        tiled=True,
    ).reshape(stretch_len, group_width)
    all_segments = lax.all_gather(segment_ids, "seq", axis=0, tiled=True)
    if span_count == seq_count:
        joined_window = lax.all_gather(joined_head, "seq", axis=0, tiled=True)
        segment_window = all_segments
        window_first = 0
    else:
        pieces = [joined_head]
        for distance in range(1, span_count):
            pieces.append(passed_along(joined_head, "seq", distance))
        joined_window = jnp.concatenate(pieces[::-1], 0)
        front_rows = (span_count - 1) * stretch_len
        segment_window = lax.dynamic_slice_in_dim(
            jnp.concatenate((jnp.zeros((front_rows,), jnp.int32), all_segments), 0),
            seq_place * stretch_len,
            span_count * stretch_len,
            0,
        )
        window_first = (seq_place - span_count + 1) * stretch_len
    key_window = joined_window[:, :group_width]
    value_window = joined_window[:, group_width:]
    key_total = span_count * stretch_len
    query_place = seq_place * stretch_len + jnp.arange(stretch_len, dtype=jnp.int32)
    key_place = window_first + jnp.arange(key_total, dtype=jnp.int32)
    allowed = (
        (segment_window[None, :] == segment_ids[:, None])
        & (key_place[None, :] <= query_place[:, None])
        & (key_place[None, :] >= 0)
    )
    queries = query_head.reshape(stretch_len, heads_here, HDIM)
    keys_all = key_window.reshape(key_total, heads_here, HDIM)
    values_all = value_window.reshape(key_total, heads_here, HDIM)
    masked = score_piece(queries, keys_all, allowed)
    row_max = jnp.max(masked, -1, keepdims=True)
    weights = jnp.where(allowed[None], jnp.exp(masked - row_max), 0.0)
    totals = jnp.sum(weights, -1)
    mixture = mix_piece(weights.astype(jnp.bfloat16), values_all)
    attention = (
        (mixture / jnp.transpose(totals)[:, :, None])
        .astype(jnp.bfloat16)
        .reshape(stretch_len, group_width)
    )
    attended_sum = lax.psum_scatter(
        jnp.dot(attention, out_weight, preferred_element_type=jnp.float32).astype(jnp.bfloat16),
        "head",
        scatter_dimension=0,
        tiled=True,
    ).astype(jnp.float32)
    middle = (residual_in.astype(jnp.float32) + residual_scale * attended_sum).astype(jnp.bfloat16)
    middle_wide = middle.astype(jnp.float32)
    mean_square = jnp.mean(middle_wide * middle_wide, -1, keepdims=True)
    normed = (middle_wide * lax.rsqrt(mean_square + norm_epsilon) * norm_gain).astype(jnp.bfloat16)
    route_count = expert_ids.shape[1]
    logits = jnp.dot(normed, router_weight, preferred_element_type=jnp.float32)
    route_hot = expert_ids[:, :, None] == jnp.arange(expert_count, dtype=jnp.int32)[None, None, :]
    chosen = jnp.sum(jnp.where(route_hot, logits[:, None, :], 0.0), -1)
    first_weight = 1.0 / (1.0 + jnp.exp(chosen[:, 1] - chosen[:, 0]))
    second_weight = 1.0 / (1.0 + jnp.exp(chosen[:, 0] - chosen[:, 1]))
    flat_hot = route_hot.reshape(tok_local * route_count, expert_count).astype(jnp.int32)
    before_count = jnp.cumsum(flat_hot, 0) - flat_hot
    route_rank = jnp.sum(before_count * flat_hot, -1)
    slot_ids = (expert_ids.reshape(-1) * CAP + route_rank).reshape(tok_local, route_count)
    slot_total = expert_count * CAP
    dispatch = jnp.any(
        slot_ids[None, :, :] == jnp.arange(slot_total, dtype=jnp.int32)[:, None, None], -1
    ).astype(jnp.bfloat16)
    packed = (
        jnp.dot(dispatch, normed, preferred_element_type=jnp.float32)
        .astype(jnp.bfloat16)
        .reshape(expert_count, CAP, D)
    )
    device_count = seq_count * head_count
    outgoing = jnp.broadcast_to(
        packed[:, None, None], (expert_count, replicas, head_count, CAP, D)
    ).reshape(device_count, CAP, D)
    arrived = lax.all_to_all(
        outgoing, ("seq", "head"), split_axis=0, concat_axis=0, tiled=True
    )
    flat_rows = arrived.reshape(device_count * CAP, D)
    gate_act = jnp.dot(flat_rows, gate_weight, preferred_element_type=jnp.float32)
    up_act = jnp.dot(flat_rows, up_weight, preferred_element_type=jnp.float32)
    hidden = (jax.nn.silu(gate_act) * up_act).astype(jnp.bfloat16)
    partial_out = lax.dot_general(
        hidden, down_weight, (((1,), (1,)), ((), ())), preferred_element_type=jnp.float32
    ).astype(jnp.bfloat16)
    returned = lax.all_to_all(
        partial_out.reshape(device_count, CAP, D),
        ("seq", "head"),
        split_axis=0,
        concat_axis=0,
        tiled=True,
    )
    by_slot = jnp.swapaxes(
        returned.reshape(expert_count, replicas * head_count, CAP, D), 1, 2
    ).reshape(slot_total, replicas * head_count, D)
    slot_range = jnp.arange(slot_total, dtype=jnp.int32)[None, :]
    first_hot = (slot_ids[:, 0:1] == slot_range).astype(jnp.bfloat16)
    second_hot = (slot_ids[:, 1:2] == slot_range).astype(jnp.bfloat16)
    first_rows = jnp.sum(
        jnp.einsum("ts,srd->trd", first_hot, by_slot, preferred_element_type=jnp.float32), 1
    )
    second_rows = jnp.sum(
        jnp.einsum("ts,srd->trd", second_hot, by_slot, preferred_element_type=jnp.float32), 1
    )
    moe_sum = first_weight[:, None] * first_rows + second_weight[:, None] * second_rows
    residual_out = (middle_wide + residual_scale * moe_sum).astype(jnp.bfloat16)
    return (residual_out, key_head, value_head)


def solution(mesh):
    return jax.shard_map(
        per_device,
        mesh=mesh,
        in_specs=(
            P(("seq", "head"), None),
            P(("seq", "head"), None),
            P(("seq", "head"), None),
            P(("seq", "head"), None),
            P(),
            P(),
            P("seq"),
            P(("seq", "head"), None),
            P(None, ("seq", "head")),
            P(None, ("seq", "head")),
            P(None, ("seq", "head")),
            P("head", None),
        ),
        out_specs=(P(("seq", "head"), None), P("seq", "head"), P("seq", "head")),
        check_vma=False,
    )
```

```python
import math

import jax
import jax.numpy as jnp
from jax import lax
from jax.sharding import PartitionSpec as P

D = 2304
HDIM = 64
LEVELS = 4
CAP = 9


residual_scale = 1.4 / math.sqrt(40.0)
norm_epsilon = 1e-05


def passed_along(value, axis, by):
    length = lax.axis_size(axis)
    pairs = [(i, i + by) for i in range(length) if 0 <= i + by < length]
    return lax.ppermute(value, axis, pairs)


def score_piece(queries, key_piece, piece_allowed):
    raw_scores = jnp.einsum(
        "qhd,khd->hqk", queries, key_piece, preferred_element_type=jnp.float32
    ) * queries.shape[2] ** (-0.5)
    return jnp.where(piece_allowed[None], raw_scores, -jnp.inf)


def mix_piece(rounded_piece, value_piece):
    return jnp.einsum(
        "hqk,khd->qhd", rounded_piece, value_piece, preferred_element_type=jnp.float32
    )


def per_device(
    query_rows,
    key_rows,
    value_rows,
    residual_in,
    norm_gain,
    router_weight,
    segment_ids,
    expert_ids,
    gate_weight,
    up_weight,
    down_weight,
    out_weight,
):
    head_count = lax.axis_size("head")
    seq_count = lax.axis_size("seq")
    tok_local = query_rows.shape[0]
    group_width = query_rows.shape[1] // head_count
    heads_here = group_width // HDIM
    stretch_len = tok_local * head_count
    span_count = min(2**LEVELS * 32 // tok_local, seq_count)
    expert_count = router_weight.shape[1]
    replicas = seq_count // expert_count
    seq_place = lax.axis_index("seq")
    joined_rows = jnp.concatenate(
        (
            key_rows.reshape(tok_local, head_count, group_width),
            value_rows.reshape(tok_local, head_count, group_width),
        ),
        2,
    )
    joined_head = lax.all_to_all(
        joined_rows, "head", split_axis=1, concat_axis=0, tiled=True
    ).reshape(stretch_len, 2 * group_width)
    key_head = joined_head[:, :group_width]
    value_head = joined_head[:, group_width:]
    query_head = lax.all_to_all(
        query_rows.reshape(tok_local, head_count, group_width),
        "head",
        split_axis=1,
        concat_axis=0,
        tiled=True,
    ).reshape(stretch_len, group_width)
    all_segments = lax.all_gather(segment_ids, "seq", axis=0, tiled=True)
    if span_count == seq_count:
        joined_window = lax.all_gather(joined_head, "seq", axis=0, tiled=True)
        segment_window = all_segments
        window_first = 0
    else:
        pieces = [joined_head]
        for distance in range(1, span_count):
            pieces.append(passed_along(joined_head, "seq", distance))
        joined_window = jnp.concatenate(pieces[::-1], 0)
        front_rows = (span_count - 1) * stretch_len
        segment_window = lax.dynamic_slice_in_dim(
            jnp.concatenate((jnp.zeros((front_rows,), jnp.int32), all_segments), 0),
            seq_place * stretch_len,
            span_count * stretch_len,
            0,
        )
        window_first = (seq_place - span_count + 1) * stretch_len
    key_window = joined_window[:, :group_width]
    value_window = joined_window[:, group_width:]
    key_total = span_count * stretch_len
    query_place = seq_place * stretch_len + jnp.arange(stretch_len, dtype=jnp.int32)
    key_place = window_first + jnp.arange(key_total, dtype=jnp.int32)
    allowed = (
        (segment_window[None, :] == segment_ids[:, None])
        & (key_place[None, :] <= query_place[:, None])
        & (key_place[None, :] >= 0)
    )
    queries = query_head.reshape(stretch_len, heads_here, HDIM)
    keys_all = key_window.reshape(key_total, heads_here, HDIM)
    values_all = value_window.reshape(key_total, heads_here, HDIM)
    masked = score_piece(queries, keys_all, allowed)
    row_max = jnp.max(masked, -1, keepdims=True)
    weights = jnp.where(allowed[None], jnp.exp(masked - row_max), 0.0)
    totals = jnp.sum(weights, -1)
    mixture = mix_piece(weights.astype(jnp.bfloat16), values_all)
    attention = (
        (mixture / jnp.transpose(totals)[:, :, None])
        .astype(jnp.bfloat16)
        .reshape(stretch_len, group_width)
    )
    attended_sum = lax.psum_scatter(
        jnp.dot(attention, out_weight, preferred_element_type=jnp.float32).astype(jnp.bfloat16),
        "head",
        scatter_dimension=0,
        tiled=True,
    ).astype(jnp.float32)
    middle = (residual_in.astype(jnp.float32) + residual_scale * attended_sum).astype(jnp.bfloat16)
    middle_wide = middle.astype(jnp.float32)
    mean_square = jnp.mean(middle_wide * middle_wide, -1, keepdims=True)
    normed = (middle_wide * lax.rsqrt(mean_square + norm_epsilon) * norm_gain).astype(jnp.bfloat16)
    route_count = expert_ids.shape[1]
    logits = jnp.dot(normed, router_weight, preferred_element_type=jnp.float32)
    route_hot = expert_ids[:, :, None] == jnp.arange(expert_count, dtype=jnp.int32)[None, None, :]
    chosen = jnp.sum(jnp.where(route_hot, logits[:, None, :], 0.0), -1)
    first_weight = 1.0 / (1.0 + jnp.exp(chosen[:, 1] - chosen[:, 0]))
    second_weight = 1.0 / (1.0 + jnp.exp(chosen[:, 0] - chosen[:, 1]))
    flat_hot = route_hot.reshape(tok_local * route_count, expert_count).astype(jnp.int32)
    before_count = jnp.cumsum(flat_hot, 0) - flat_hot
    route_rank = jnp.sum(before_count * flat_hot, -1)
    slot_ids = (expert_ids.reshape(-1) * CAP + route_rank).reshape(tok_local, route_count)
    slot_total = expert_count * CAP
    dispatch = jnp.any(
        slot_ids[None, :, :] == jnp.arange(slot_total, dtype=jnp.int32)[:, None, None], -1
    ).astype(jnp.bfloat16)
    packed = (
        jnp.dot(dispatch, normed, preferred_element_type=jnp.float32)
        .astype(jnp.bfloat16)
        .reshape(expert_count, CAP, D)
    )
    outgoing = jnp.broadcast_to(packed[:, None], (expert_count, replicas, CAP, D)).reshape(
        seq_count, CAP, D
    )
    arrived = lax.all_to_all(outgoing, "seq", split_axis=0, concat_axis=0, tiled=True)
    slot_count = arrived.shape[1]
    flat_rows = arrived.reshape(seq_count * slot_count, D)
    group_rows = lax.all_gather(flat_rows, "head", axis=0, tiled=True)
    gate_act = jnp.dot(group_rows, gate_weight, preferred_element_type=jnp.float32)
    up_act = jnp.dot(group_rows, up_weight, preferred_element_type=jnp.float32)
    hidden = (jax.nn.silu(gate_act) * up_act).astype(jnp.bfloat16)
    partial_out = lax.dot_general(
        hidden, down_weight, (((1,), (1,)), ((), ())), preferred_element_type=jnp.float32
    ).astype(jnp.bfloat16)
    shard_out = lax.psum_scatter(partial_out, "head", scatter_dimension=0, tiled=True)
    returned = lax.all_to_all(
        shard_out.reshape(seq_count, slot_count, D), "seq", split_axis=0, concat_axis=0, tiled=True
    )
    by_slot = jnp.swapaxes(returned.reshape(expert_count, replicas, CAP, D), 1, 2).reshape(
        slot_total, replicas, D
    )
    slot_range = jnp.arange(slot_total, dtype=jnp.int32)[None, :]
    first_hot = (slot_ids[:, 0:1] == slot_range).astype(jnp.bfloat16)
    second_hot = (slot_ids[:, 1:2] == slot_range).astype(jnp.bfloat16)
    first_rows = jnp.sum(
        jnp.einsum("ts,srd->trd", first_hot, by_slot, preferred_element_type=jnp.float32), 1
    )
    second_rows = jnp.sum(
        jnp.einsum("ts,srd->trd", second_hot, by_slot, preferred_element_type=jnp.float32), 1
    )
    moe_sum = first_weight[:, None] * first_rows + second_weight[:, None] * second_rows
    residual_out = (middle_wide + residual_scale * moe_sum).astype(jnp.bfloat16)
    return (residual_out, key_head, value_head)


def solution(mesh):
    return jax.shard_map(
        per_device,
        mesh=mesh,
        in_specs=(
            P(("seq", "head"), None),
            P(("seq", "head"), None),
            P(("seq", "head"), None),
            P(("seq", "head"), None),
            P(),
            P(),
            P("seq"),
            P(("seq", "head"), None),
            P(None, ("seq", "head")),
            P(None, ("seq", "head")),
            P(None, ("seq", "head")),
            P("head", None),
        ),
        out_specs=(P(("seq", "head"), None), P("seq", "head"), P("seq", "head")),
        check_vma=False,
    )
```

```python
import math

import jax
import jax.numpy as jnp
from jax import lax
from jax.sharding import PartitionSpec as P

D = 2304
HDIM = 64
LEVELS = 4
CAP = 9


residual_scale = 1.4 / math.sqrt(40.0)
norm_epsilon = 1e-05


def passed_along(value, axis, by):
    length = lax.axis_size(axis)
    pairs = [(i, i + by) for i in range(length) if 0 <= i + by < length]
    return lax.ppermute(value, axis, pairs)


def score_piece(queries, key_piece, piece_allowed):
    raw_scores = jnp.einsum(
        "qhd,khd->hqk", queries, key_piece, preferred_element_type=jnp.float32
    ) * queries.shape[2] ** (-0.5)
    return jnp.where(piece_allowed[None], raw_scores, -jnp.inf)


def mix_piece(rounded_piece, value_piece):
    return jnp.einsum(
        "hqk,khd->qhd", rounded_piece, value_piece, preferred_element_type=jnp.float32
    )


def per_device(
    query_rows,
    key_rows,
    value_rows,
    residual_in,
    norm_gain,
    router_weight,
    segment_ids,
    expert_ids,
    gate_weight,
    up_weight,
    down_weight,
    out_weight,
):
    head_count = lax.axis_size("head")
    seq_count = lax.axis_size("seq")
    tok_local = query_rows.shape[0]
    group_width = query_rows.shape[1] // head_count
    heads_here = group_width // HDIM
    stretch_len = tok_local * head_count
    span_count = min(2**LEVELS * 32 // tok_local, seq_count)
    expert_count = router_weight.shape[1]
    replicas = seq_count // expert_count
    seq_place = lax.axis_index("seq")
    joined_rows = jnp.concatenate(
        (
            key_rows.reshape(tok_local, head_count, group_width),
            value_rows.reshape(tok_local, head_count, group_width),
        ),
        2,
    )
    joined_head = lax.all_to_all(
        joined_rows, "head", split_axis=1, concat_axis=0, tiled=True
    ).reshape(stretch_len, 2 * group_width)
    key_head = joined_head[:, :group_width]
    value_head = joined_head[:, group_width:]
    query_head = lax.all_to_all(
        query_rows.reshape(tok_local, head_count, group_width),
        "head",
        split_axis=1,
        concat_axis=0,
        tiled=True,
    ).reshape(stretch_len, group_width)
    all_segments = lax.all_gather(segment_ids, "seq", axis=0, tiled=True)
    if span_count == seq_count:
        joined_window = lax.all_gather(joined_head, "seq", axis=0, tiled=True)
        segment_window = all_segments
        window_first = 0
    else:
        pieces = [joined_head]
        for distance in range(1, span_count):
            pieces.append(passed_along(joined_head, "seq", distance))
        joined_window = jnp.concatenate(pieces[::-1], 0)
        front_rows = (span_count - 1) * stretch_len
        segment_window = lax.dynamic_slice_in_dim(
            jnp.concatenate((jnp.zeros((front_rows,), jnp.int32), all_segments), 0),
            seq_place * stretch_len,
            span_count * stretch_len,
            0,
        )
        window_first = (seq_place - span_count + 1) * stretch_len
    key_window = joined_window[:, :group_width]
    value_window = joined_window[:, group_width:]
    key_total = span_count * stretch_len
    query_place = seq_place * stretch_len + jnp.arange(stretch_len, dtype=jnp.int32)
    key_place = window_first + jnp.arange(key_total, dtype=jnp.int32)
    allowed = (
        (segment_window[None, :] == segment_ids[:, None])
        & (key_place[None, :] <= query_place[:, None])
        & (key_place[None, :] >= 0)
    )
    queries = query_head.reshape(stretch_len, heads_here, HDIM)
    keys_all = key_window.reshape(key_total, heads_here, HDIM)
    values_all = value_window.reshape(key_total, heads_here, HDIM)
    masked = score_piece(queries, keys_all, allowed)
    row_max = jnp.max(masked, -1, keepdims=True)
    weights = jnp.where(allowed[None], jnp.exp(masked - row_max), 0.0)
    totals = jnp.sum(weights, -1)
    mixture = mix_piece(weights.astype(jnp.bfloat16), values_all)
    attention = (
        (mixture / jnp.transpose(totals)[:, :, None])
        .astype(jnp.bfloat16)
        .reshape(stretch_len, group_width)
    )
    attended_sum = lax.psum_scatter(
        jnp.dot(attention, out_weight, preferred_element_type=jnp.float32).astype(jnp.bfloat16),
        "head",
        scatter_dimension=0,
        tiled=True,
    ).astype(jnp.float32)
    middle = (residual_in.astype(jnp.float32) + residual_scale * attended_sum).astype(jnp.bfloat16)
    middle_wide = middle.astype(jnp.float32)
    mean_square = jnp.mean(middle_wide * middle_wide, -1, keepdims=True)
    normed = (middle_wide * lax.rsqrt(mean_square + norm_epsilon) * norm_gain).astype(jnp.bfloat16)
    route_count = expert_ids.shape[1]
    logits = jnp.dot(normed, router_weight, preferred_element_type=jnp.float32)
    route_hot = expert_ids[:, :, None] == jnp.arange(expert_count, dtype=jnp.int32)[None, None, :]
    chosen = jnp.sum(jnp.where(route_hot, logits[:, None, :], 0.0), -1)
    first_weight = 1.0 / (1.0 + jnp.exp(chosen[:, 1] - chosen[:, 0]))
    second_weight = 1.0 / (1.0 + jnp.exp(chosen[:, 0] - chosen[:, 1]))
    flat_hot = route_hot.reshape(tok_local * route_count, expert_count).astype(jnp.int32)
    before_count = jnp.cumsum(flat_hot, 0) - flat_hot
    route_rank = jnp.sum(before_count * flat_hot, -1)
    slot_ids = (expert_ids.reshape(-1) * CAP + route_rank).reshape(tok_local, route_count)
    slot_total = expert_count * CAP
    slot_grid = jnp.arange(slot_total, dtype=jnp.int32).reshape(expert_count, CAP)
    dispatch = jnp.any(
        slot_ids[None, None, :, :] == slot_grid[:, :, None, None], -1
    ).astype(jnp.bfloat16)
    packed = jnp.einsum(
        "ect,td->ecd", dispatch, normed, preferred_element_type=jnp.float32
    ).astype(jnp.bfloat16)
    outgoing = jnp.broadcast_to(packed[:, None], (expert_count, replicas, CAP, D)).reshape(
        seq_count, CAP, D
    )
    arrived = lax.all_to_all(outgoing, "seq", split_axis=0, concat_axis=0, tiled=True)
    group_rows = lax.all_gather(arrived, "head", axis=0, tiled=True)
    gate_act = jnp.einsum(
        "rcd,df->rcf", group_rows, gate_weight, preferred_element_type=jnp.float32
    )
    up_act = jnp.einsum("rcd,df->rcf", group_rows, up_weight, preferred_element_type=jnp.float32)
    hidden = (jax.nn.silu(gate_act) * up_act).astype(jnp.bfloat16)
    partial_out = jnp.einsum(
        "rcf,df->rcd", hidden, down_weight, preferred_element_type=jnp.float32
    ).astype(jnp.bfloat16)
    shard_out = lax.psum_scatter(partial_out, "head", scatter_dimension=0, tiled=True)
    returned = lax.all_to_all(shard_out, "seq", split_axis=0, concat_axis=0, tiled=True)
    by_expert = returned.reshape(expert_count, replicas, CAP, D)
    first_hot = (slot_ids[:, 0, None, None] == slot_grid[None]).astype(jnp.bfloat16)
    second_hot = (slot_ids[:, 1, None, None] == slot_grid[None]).astype(jnp.bfloat16)
    first_rows = jnp.sum(
        jnp.einsum("tec,ercd->trd", first_hot, by_expert, preferred_element_type=jnp.float32), 1
    )
    second_rows = jnp.sum(
        jnp.einsum("tec,ercd->trd", second_hot, by_expert, preferred_element_type=jnp.float32), 1
    )
    moe_sum = first_weight[:, None] * first_rows + second_weight[:, None] * second_rows
    residual_out = (middle_wide + residual_scale * moe_sum).astype(jnp.bfloat16)
    return (residual_out, key_head, value_head)


def solution(mesh):
    return jax.shard_map(
        per_device,
        mesh=mesh,
        in_specs=(
            P(("seq", "head"), None),
            P(("seq", "head"), None),
            P(("seq", "head"), None),
            P(("seq", "head"), None),
            P(),
            P(),
            P("seq"),
            P(("seq", "head"), None),
            P(None, ("seq", "head")),
            P(None, ("seq", "head")),
            P(None, ("seq", "head")),
            P("head", None),
        ),
        out_specs=(P(("seq", "head"), None), P("seq", "head"), P("seq", "head")),
        check_vma=False,
    )
```

```python
import math

import jax
import jax.numpy as jnp
from jax import lax
from jax.experimental.layout import Layout, with_layout_constraint
from jax.sharding import PartitionSpec as P

D = 2304
HDIM = 64
LEVELS = 4
CAP = 9


residual_scale = 1.4 / math.sqrt(40.0)
norm_epsilon = 1e-05


def passed_along(value, axis, by):
    length = lax.axis_size(axis)
    pairs = [(i, i + by) for i in range(length) if 0 <= i + by < length]
    return lax.ppermute(value, axis, pairs)


def score_piece(queries, key_piece, piece_allowed):
    raw_scores = jnp.einsum(
        "qhd,hdk->hqk", queries, key_piece, preferred_element_type=jnp.float32
    ) * queries.shape[2] ** (-0.5)
    return jnp.where(piece_allowed[None], raw_scores, -jnp.inf)


def mix_piece(rounded_piece, value_piece):
    return jnp.einsum(
        "hqk,hdk->qhd", rounded_piece, value_piece, preferred_element_type=jnp.float32
    )


def per_device(
    query_rows,
    key_rows,
    value_rows,
    residual_in,
    norm_gain,
    router_weight,
    segment_ids,
    expert_ids,
    gate_weight,
    up_weight,
    down_weight,
    out_weight,
):
    head_count = lax.axis_size("head")
    seq_count = lax.axis_size("seq")
    tok_local = query_rows.shape[0]
    group_width = query_rows.shape[1] // head_count
    heads_here = group_width // HDIM
    stretch_len = tok_local * head_count
    span_count = min(2**LEVELS * 32 // tok_local, seq_count)
    expert_count = router_weight.shape[1]
    replicas = seq_count // expert_count
    seq_place = lax.axis_index("seq")
    joined_rows_t = jnp.concatenate(
        (
            jnp.transpose(key_rows).reshape(head_count, group_width, tok_local),
            jnp.transpose(value_rows).reshape(head_count, group_width, tok_local),
        ),
        1,
    )
    joined_head_t = lax.all_to_all(
        joined_rows_t, "head", split_axis=0, concat_axis=2, tiled=True
    ).reshape(2 * group_width, stretch_len)
    joined_head_t = with_layout_constraint(joined_head_t, Layout(major_to_minor=(0, 1)))
    key_head = jnp.transpose(joined_head_t[:group_width])
    value_head = jnp.transpose(joined_head_t[group_width:])
    query_head = lax.all_to_all(
        query_rows.reshape(tok_local, head_count, group_width),
        "head",
        split_axis=1,
        concat_axis=0,
        tiled=True,
    ).reshape(stretch_len, group_width)
    all_segments = lax.all_gather(segment_ids, "seq", axis=0, tiled=True)
    if span_count == seq_count:
        joined_window_t = lax.all_gather(joined_head_t, "seq", axis=1, tiled=True)
        segment_window = all_segments
        window_first = 0
    else:
        pieces = [joined_head_t]
        for distance in range(1, span_count):
            pieces.append(passed_along(joined_head_t, "seq", distance))
        joined_window_t = jnp.concatenate(pieces[::-1], 1)
        front_rows = (span_count - 1) * stretch_len
        segment_window = lax.dynamic_slice_in_dim(
            jnp.concatenate((jnp.zeros((front_rows,), jnp.int32), all_segments), 0),
            seq_place * stretch_len,
            span_count * stretch_len,
            0,
        )
        window_first = (seq_place - span_count + 1) * stretch_len
    key_total = span_count * stretch_len
    joined_window_t = with_layout_constraint(joined_window_t, Layout(major_to_minor=(0, 1)))
    keys_t = joined_window_t[:group_width].reshape(heads_here, HDIM, key_total)
    values_t = joined_window_t[group_width:].reshape(heads_here, HDIM, key_total)
    query_place = seq_place * stretch_len + jnp.arange(stretch_len, dtype=jnp.int32)
    key_place = window_first + jnp.arange(key_total, dtype=jnp.int32)
    allowed = (
        (segment_window[None, :] == segment_ids[:, None])
        & (key_place[None, :] <= query_place[:, None])
        & (key_place[None, :] >= 0)
    )
    queries = query_head.reshape(stretch_len, heads_here, HDIM)
    masked = score_piece(queries, keys_t, allowed)
    row_max = jnp.max(masked, -1, keepdims=True)
    weights = jnp.where(allowed[None], jnp.exp(masked - row_max), 0.0)
    totals = jnp.sum(weights, -1)
    mixture = mix_piece(weights.astype(jnp.bfloat16), values_t)
    attention = (
        (mixture / jnp.transpose(totals)[:, :, None])
        .astype(jnp.bfloat16)
        .reshape(stretch_len, group_width)
    )
    attended_sum = lax.psum_scatter(
        jnp.dot(attention, out_weight, preferred_element_type=jnp.float32).astype(jnp.bfloat16),
        "head",
        scatter_dimension=0,
        tiled=True,
    ).astype(jnp.float32)
    middle = (residual_in.astype(jnp.float32) + residual_scale * attended_sum).astype(jnp.bfloat16)
    middle_wide = middle.astype(jnp.float32)
    mean_square = jnp.mean(middle_wide * middle_wide, -1, keepdims=True)
    normed = (middle_wide * lax.rsqrt(mean_square + norm_epsilon) * norm_gain).astype(jnp.bfloat16)
    route_count = expert_ids.shape[1]
    logits = jnp.dot(normed, router_weight, preferred_element_type=jnp.float32)
    route_hot = expert_ids[:, :, None] == jnp.arange(expert_count, dtype=jnp.int32)[None, None, :]
    chosen = jnp.sum(jnp.where(route_hot, logits[:, None, :], 0.0), -1)
    first_weight = 1.0 / (1.0 + jnp.exp(chosen[:, 1] - chosen[:, 0]))
    second_weight = 1.0 / (1.0 + jnp.exp(chosen[:, 0] - chosen[:, 1]))
    flat_hot = route_hot.reshape(tok_local * route_count, expert_count).astype(jnp.int32)
    before_count = jnp.cumsum(flat_hot, 0) - flat_hot
    route_rank = jnp.sum(before_count * flat_hot, -1)
    slot_ids = (expert_ids.reshape(-1) * CAP + route_rank).reshape(tok_local, route_count)
    slot_total = expert_count * CAP
    slot_grid = jnp.arange(slot_total, dtype=jnp.int32).reshape(expert_count, CAP)
    dispatch = jnp.any(
        slot_ids[None, None, :, :] == slot_grid[:, :, None, None], -1
    ).astype(jnp.bfloat16)
    packed = jnp.einsum(
        "ect,td->ecd", dispatch, normed, preferred_element_type=jnp.float32
    ).astype(jnp.bfloat16)
    outgoing = jnp.broadcast_to(packed[:, None], (expert_count, replicas, CAP, D)).reshape(
        seq_count, CAP, D
    )
    arrived = lax.all_to_all(outgoing, "seq", split_axis=0, concat_axis=0, tiled=True)
    group_rows = lax.all_gather(arrived, "head", axis=0, tiled=True)
    gate_act = jnp.einsum(
        "rcd,df->rcf", group_rows, gate_weight, preferred_element_type=jnp.float32
    )
    up_act = jnp.einsum("rcd,df->rcf", group_rows, up_weight, preferred_element_type=jnp.float32)
    hidden = (jax.nn.silu(gate_act) * up_act).astype(jnp.bfloat16)
    partial_out = jnp.einsum(
        "rcf,df->rcd", hidden, down_weight, preferred_element_type=jnp.float32
    ).astype(jnp.bfloat16)
    shard_out = lax.psum_scatter(partial_out, "head", scatter_dimension=0, tiled=True)
    returned = lax.all_to_all(shard_out, "seq", split_axis=0, concat_axis=0, tiled=True)
    by_expert = returned.reshape(expert_count, replicas, CAP, D)
    first_hot = (slot_ids[:, 0, None, None] == slot_grid[None]).astype(jnp.bfloat16)
    second_hot = (slot_ids[:, 1, None, None] == slot_grid[None]).astype(jnp.bfloat16)
    first_rows = jnp.sum(
        jnp.einsum("tec,ercd->trd", first_hot, by_expert, preferred_element_type=jnp.float32), 1
    )
    second_rows = jnp.sum(
        jnp.einsum("tec,ercd->trd", second_hot, by_expert, preferred_element_type=jnp.float32), 1
    )
    moe_sum = first_weight[:, None] * first_rows + second_weight[:, None] * second_rows
    residual_out = (middle_wide + residual_scale * moe_sum).astype(jnp.bfloat16)
    return (residual_out, key_head, value_head)


def solution(mesh):
    return jax.shard_map(
        per_device,
        mesh=mesh,
        in_specs=(
            P(("seq", "head"), None),
            P(("seq", "head"), None),
            P(("seq", "head"), None),
            P(("seq", "head"), None),
            P(),
            P(),
            P("seq"),
            P(("seq", "head"), None),
            P(None, ("seq", "head")),
            P(None, ("seq", "head")),
            P(None, ("seq", "head")),
            P("head", None),
        ),
        out_specs=(P(("seq", "head"), None), P("seq", "head"), P("seq", "head")),
        check_vma=False,
    )
```

```python
import math

import jax
import jax.numpy as jnp
from jax import lax
from jax.experimental.layout import Layout, with_layout_constraint
from jax.sharding import PartitionSpec as P

D = 2304
HDIM = 64
LEVELS = 4
CAP = 9


residual_scale = 1.4 / math.sqrt(40.0)
norm_epsilon = 1e-05


def passed_along(value, axis, by):
    length = lax.axis_size(axis)
    pairs = [(i, i + by) for i in range(length) if 0 <= i + by < length]
    return lax.ppermute(value, axis, pairs)


def score_piece(queries, key_piece, piece_allowed):
    raw_scores = jnp.einsum(
        "qhd,hdk->hqk", queries, key_piece, preferred_element_type=jnp.float32
    ) * queries.shape[2] ** (-0.5)
    return jnp.where(piece_allowed[None], raw_scores, -jnp.inf)


def mix_piece(rounded_piece, value_piece):
    return jnp.einsum(
        "hqk,hdk->qhd", rounded_piece, value_piece, preferred_element_type=jnp.float32
    )


def per_device(
    query_rows,
    key_rows,
    value_rows,
    residual_in,
    norm_gain,
    router_weight,
    segment_ids,
    expert_ids,
    gate_weight,
    up_weight,
    down_weight,
    out_weight,
):
    head_count = lax.axis_size("head")
    seq_count = lax.axis_size("seq")
    tok_local = query_rows.shape[0]
    group_width = query_rows.shape[1] // head_count
    heads_here = group_width // HDIM
    stretch_len = tok_local * head_count
    span_count = min(2**LEVELS * 32 // tok_local, seq_count)
    expert_count = router_weight.shape[1]
    replicas = seq_count // expert_count
    seq_place = lax.axis_index("seq")
    joined_rows_t = jnp.concatenate(
        (
            jnp.transpose(key_rows).reshape(head_count, group_width, tok_local),
            jnp.transpose(value_rows).reshape(head_count, group_width, tok_local),
        ),
        1,
    )
    joined_head_t = lax.all_to_all(
        joined_rows_t, "head", split_axis=0, concat_axis=2, tiled=True
    ).reshape(2 * group_width, stretch_len)
    joined_head_t = with_layout_constraint(joined_head_t, Layout(major_to_minor=(0, 1)))
    key_head = jnp.transpose(joined_head_t[:group_width])
    value_head = jnp.transpose(joined_head_t[group_width:])
    query_head = lax.all_to_all(
        query_rows.reshape(tok_local, head_count, group_width),
        "head",
        split_axis=1,
        concat_axis=0,
        tiled=True,
    ).reshape(stretch_len, group_width)
    all_segments = lax.all_gather(segment_ids, "seq", axis=0, tiled=True)
    if span_count == seq_count:
        joined_window_t = lax.all_gather(joined_head_t, "seq", axis=1, tiled=True)
        segment_window = all_segments
        window_first = 0
    else:
        pieces = [joined_head_t]
        for distance in range(1, span_count):
            pieces.append(passed_along(joined_head_t, "seq", distance))
        joined_window_t = jnp.concatenate(pieces[::-1], 1)
        front_rows = (span_count - 1) * stretch_len
        segment_window = lax.dynamic_slice_in_dim(
            jnp.concatenate((jnp.zeros((front_rows,), jnp.int32), all_segments), 0),
            seq_place * stretch_len,
            span_count * stretch_len,
            0,
        )
        window_first = (seq_place - span_count + 1) * stretch_len
    key_total = span_count * stretch_len
    joined_window_t = with_layout_constraint(joined_window_t, Layout(major_to_minor=(0, 1)))
    keys_t = joined_window_t[:group_width].reshape(heads_here, HDIM, key_total)
    values_t = joined_window_t[group_width:].reshape(heads_here, HDIM, key_total)
    query_place = seq_place * stretch_len + jnp.arange(stretch_len, dtype=jnp.int32)
    key_place = window_first + jnp.arange(key_total, dtype=jnp.int32)
    allowed = (
        (segment_window[None, :] == segment_ids[:, None])
        & (key_place[None, :] <= query_place[:, None])
        & (key_place[None, :] >= 0)
    )
    queries = query_head.reshape(stretch_len, heads_here, HDIM)
    masked = score_piece(queries, keys_t, allowed)
    row_max = jnp.max(masked, -1, keepdims=True)
    weights = jnp.where(allowed[None], jnp.exp(masked - row_max), 0.0)
    totals = jnp.sum(weights, -1)
    mixture = mix_piece(weights.astype(jnp.bfloat16), values_t)
    attention = (
        (mixture / jnp.transpose(totals)[:, :, None])
        .astype(jnp.bfloat16)
        .reshape(stretch_len, group_width)
    )
    attended_sum = lax.psum_scatter(
        jnp.dot(attention, out_weight, preferred_element_type=jnp.float32).astype(jnp.bfloat16),
        "head",
        scatter_dimension=0,
        tiled=True,
    ).astype(jnp.float32)
    middle = (residual_in.astype(jnp.float32) + residual_scale * attended_sum).astype(jnp.bfloat16)
    middle_wide = middle.astype(jnp.float32)
    mean_square = jnp.mean(middle_wide * middle_wide, -1, keepdims=True)
    normed = (middle_wide * lax.rsqrt(mean_square + norm_epsilon) * norm_gain).astype(jnp.bfloat16)
    route_count = expert_ids.shape[1]
    logits = jnp.dot(normed, router_weight, preferred_element_type=jnp.float32)
    route_hot = expert_ids[:, :, None] == jnp.arange(expert_count, dtype=jnp.int32)[None, None, :]
    chosen = jnp.sum(jnp.where(route_hot, logits[:, None, :], 0.0), -1)
    first_weight = 1.0 / (1.0 + jnp.exp(chosen[:, 1] - chosen[:, 0]))
    second_weight = 1.0 / (1.0 + jnp.exp(chosen[:, 0] - chosen[:, 1]))
    flat_hot = route_hot.reshape(tok_local * route_count, expert_count).astype(jnp.int32)
    before_count = jnp.cumsum(flat_hot, 0) - flat_hot
    route_rank = jnp.sum(before_count * flat_hot, -1)
    slot_ids = (expert_ids.reshape(-1) * CAP + route_rank).reshape(tok_local, route_count)
    slot_total = expert_count * CAP
    slot_grid = jnp.arange(slot_total, dtype=jnp.int32).reshape(expert_count, CAP)
    dispatch = jnp.any(
        slot_ids[None, None, :, :] == slot_grid[:, :, None, None], -1
    ).astype(jnp.bfloat16)
    packed = jnp.einsum(
        "ect,td->ecd", dispatch, normed, preferred_element_type=jnp.float32
    ).astype(jnp.bfloat16)
    outgoing = jnp.broadcast_to(packed[:, None], (expert_count, replicas, CAP, D)).reshape(
        seq_count, CAP, D
    )
    arrived = lax.all_to_all(outgoing, "seq", split_axis=0, concat_axis=0, tiled=True)
    group_rows = lax.all_gather(jnp.swapaxes(arrived, 0, 1), "head", axis=0, tiled=False)
    gate_act = jnp.einsum(
        "hcsd,df->hcsf", group_rows, gate_weight, preferred_element_type=jnp.float32
    )
    up_act = jnp.einsum(
        "hcsd,df->hcsf", group_rows, up_weight, preferred_element_type=jnp.float32
    )
    hidden = (jax.nn.silu(gate_act) * up_act).astype(jnp.bfloat16)
    partial_out = jnp.einsum(
        "hcsf,df->hcsd", hidden, down_weight, preferred_element_type=jnp.float32
    ).astype(jnp.bfloat16)
    shard_out = jnp.swapaxes(
        lax.psum_scatter(partial_out, "head", scatter_dimension=0, tiled=False), 0, 1
    )
    returned = lax.all_to_all(shard_out, "seq", split_axis=0, concat_axis=0, tiled=True)
    by_expert = returned.reshape(expert_count, replicas, CAP, D)
    first_hot = (slot_ids[:, 0, None, None] == slot_grid[None]).astype(jnp.bfloat16)
    second_hot = (slot_ids[:, 1, None, None] == slot_grid[None]).astype(jnp.bfloat16)
    first_rows = jnp.sum(
        jnp.einsum("tec,ercd->trd", first_hot, by_expert, preferred_element_type=jnp.float32), 1
    )
    second_rows = jnp.sum(
        jnp.einsum("tec,ercd->trd", second_hot, by_expert, preferred_element_type=jnp.float32), 1
    )
    moe_sum = first_weight[:, None] * first_rows + second_weight[:, None] * second_rows
    residual_out = (middle_wide + residual_scale * moe_sum).astype(jnp.bfloat16)
    return (residual_out, key_head, value_head)


def solution(mesh):
    return jax.shard_map(
        per_device,
        mesh=mesh,
        in_specs=(
            P(("seq", "head"), None),
            P(("seq", "head"), None),
            P(("seq", "head"), None),
            P(("seq", "head"), None),
            P(),
            P(),
            P("seq"),
            P(("seq", "head"), None),
            P(None, ("seq", "head")),
            P(None, ("seq", "head")),
            P(None, ("seq", "head")),
            P("head", None),
        ),
        out_specs=(P(("seq", "head"), None), P("seq", "head"), P("seq", "head")),
        check_vma=False,
    )
```

```python
import math

import jax
import jax.numpy as jnp
from jax import lax
from jax.experimental import pallas as pl
from jax.experimental.layout import Layout, with_layout_constraint
from jax.sharding import PartitionSpec as P

D = 2304
HDIM = 64
LEVELS = 4
CAP = 9


residual_scale = 1.4 / math.sqrt(40.0)
norm_epsilon = 1e-05


def passed_along(value, axis, by):
    length = lax.axis_size(axis)
    pairs = [(i, i + by) for i in range(length) if 0 <= i + by < length]
    return lax.ppermute(value, axis, pairs)


def score_piece(queries, key_piece, piece_allowed):
    raw_scores = jnp.einsum(
        "qhd,hdk->hqk", queries, key_piece, preferred_element_type=jnp.float32
    ) * queries.shape[2] ** (-0.5)
    return jnp.where(piece_allowed[None], raw_scores, -jnp.inf)


def mix_piece(rounded_piece, value_piece):
    return jnp.einsum(
        "hqk,hdk->qhd", rounded_piece, value_piece, preferred_element_type=jnp.float32
    )


def attention_project(q3, window_t, allowed, out_weight):
    heads, tokens, _ = q3.shape
    group_width = heads * HDIM

    def kernel(q_ref, window_ref, allowed_ref, weight_ref, out_ref):
        allowed_now = allowed_ref[...] != 0
        total = jnp.zeros(out_ref.shape, jnp.float32)
        for head in range(heads):
            keys = window_ref[pl.ds(head * HDIM, HDIM), :]
            values = window_ref[pl.ds(group_width + head * HDIM, HDIM), :]
            raw = jnp.dot(q_ref[head], keys, preferred_element_type=jnp.float32) * HDIM ** (-0.5)
            masked = jnp.where(allowed_now, raw, -jnp.inf)
            top = jnp.max(masked, axis=1, keepdims=True)
            weights = jnp.where(allowed_now, jnp.exp(masked - top), 0.0)
            sums = jnp.sum(weights, axis=1, keepdims=True)
            mixed = lax.dot_general(
                weights.astype(jnp.bfloat16),
                values,
                (((1,), (1,)), ((), ())),
                preferred_element_type=jnp.float32,
            )
            attended = (mixed / sums).astype(jnp.bfloat16)
            total = total + jnp.dot(
                attended,
                weight_ref[pl.ds(head * HDIM, HDIM), :],
                preferred_element_type=jnp.float32,
            )
        out_ref[...] = total.astype(out_ref.dtype)

    return pl.pallas_call(
        kernel, out_shape=jax.ShapeDtypeStruct((tokens, out_weight.shape[1]), jnp.bfloat16)
    )(q3, window_t, allowed.astype(jnp.int32), out_weight)


def per_device(
    query_rows,
    key_rows,
    value_rows,
    residual_in,
    norm_gain,
    router_weight,
    segment_ids,
    expert_ids,
    gate_weight,
    up_weight,
    down_weight,
    out_weight,
):
    head_count = lax.axis_size("head")
    seq_count = lax.axis_size("seq")
    tok_local = query_rows.shape[0]
    group_width = query_rows.shape[1] // head_count
    heads_here = group_width // HDIM
    stretch_len = tok_local * head_count
    span_count = min(2**LEVELS * 32 // tok_local, seq_count)
    expert_count = router_weight.shape[1]
    replicas = seq_count // expert_count
    seq_place = lax.axis_index("seq")
    joined_rows_t = jnp.concatenate(
        (
            jnp.transpose(key_rows).reshape(head_count, group_width, tok_local),
            jnp.transpose(value_rows).reshape(head_count, group_width, tok_local),
        ),
        1,
    )
    joined_head_t = lax.all_to_all(
        joined_rows_t, "head", split_axis=0, concat_axis=2, tiled=True
    ).reshape(2 * group_width, stretch_len)
    joined_head_t = with_layout_constraint(joined_head_t, Layout(major_to_minor=(0, 1)))
    key_head = jnp.transpose(joined_head_t[:group_width])
    value_head = jnp.transpose(joined_head_t[group_width:])
    query_head = lax.all_to_all(
        query_rows.reshape(tok_local, head_count, group_width),
        "head",
        split_axis=1,
        concat_axis=0,
        tiled=True,
    ).reshape(stretch_len, group_width)
    all_segments = lax.all_gather(segment_ids, "seq", axis=0, tiled=True)
    if span_count == seq_count:
        joined_window_t = lax.all_gather(joined_head_t, "seq", axis=1, tiled=True)
        segment_window = all_segments
        window_first = 0
    else:
        pieces = [joined_head_t]
        for distance in range(1, span_count):
            pieces.append(passed_along(joined_head_t, "seq", distance))
        joined_window_t = jnp.concatenate(pieces[::-1], 1)
        front_rows = (span_count - 1) * stretch_len
        segment_window = lax.dynamic_slice_in_dim(
            jnp.concatenate((jnp.zeros((front_rows,), jnp.int32), all_segments), 0),
            seq_place * stretch_len,
            span_count * stretch_len,
            0,
        )
        window_first = (seq_place - span_count + 1) * stretch_len
    key_total = span_count * stretch_len
    joined_window_t = with_layout_constraint(joined_window_t, Layout(major_to_minor=(0, 1)))
    query_place = seq_place * stretch_len + jnp.arange(stretch_len, dtype=jnp.int32)
    key_place = window_first + jnp.arange(key_total, dtype=jnp.int32)
    allowed = (
        (segment_window[None, :] == segment_ids[:, None])
        & (key_place[None, :] <= query_place[:, None])
        & (key_place[None, :] >= 0)
    )
    queries = jnp.transpose(query_head.reshape(stretch_len, heads_here, HDIM), (1, 0, 2))
    attended_sum = lax.psum_scatter(
        attention_project(queries, joined_window_t, allowed, out_weight),
        "head",
        scatter_dimension=0,
        tiled=True,
    ).astype(jnp.float32)
    middle = (residual_in.astype(jnp.float32) + residual_scale * attended_sum).astype(jnp.bfloat16)
    middle_wide = middle.astype(jnp.float32)
    mean_square = jnp.mean(middle_wide * middle_wide, -1, keepdims=True)
    normed = (middle_wide * lax.rsqrt(mean_square + norm_epsilon) * norm_gain).astype(jnp.bfloat16)
    route_count = expert_ids.shape[1]
    logits = jnp.dot(normed, router_weight, preferred_element_type=jnp.float32)
    route_hot = expert_ids[:, :, None] == jnp.arange(expert_count, dtype=jnp.int32)[None, None, :]
    chosen = jnp.sum(jnp.where(route_hot, logits[:, None, :], 0.0), -1)
    first_weight = 1.0 / (1.0 + jnp.exp(chosen[:, 1] - chosen[:, 0]))
    second_weight = 1.0 / (1.0 + jnp.exp(chosen[:, 0] - chosen[:, 1]))
    flat_hot = route_hot.reshape(tok_local * route_count, expert_count).astype(jnp.int32)
    before_count = jnp.cumsum(flat_hot, 0) - flat_hot
    route_rank = jnp.sum(before_count * flat_hot, -1)
    slot_ids = (expert_ids.reshape(-1) * CAP + route_rank).reshape(tok_local, route_count)
    slot_total = expert_count * CAP
    slot_grid = jnp.arange(slot_total, dtype=jnp.int32).reshape(expert_count, CAP)
    dispatch = jnp.any(
        slot_ids[None, None, :, :] == slot_grid[:, :, None, None], -1
    ).astype(jnp.bfloat16)
    packed = jnp.einsum(
        "ect,td->ecd", dispatch, normed, preferred_element_type=jnp.float32
    ).astype(jnp.bfloat16)
    outgoing = jnp.broadcast_to(packed[:, None], (expert_count, replicas, CAP, D)).reshape(
        seq_count, CAP, D
    )
    arrived = lax.all_to_all(outgoing, "seq", split_axis=0, concat_axis=0, tiled=True)
    group_rows = lax.all_gather(jnp.swapaxes(arrived, 0, 1), "head", axis=0, tiled=False)
    gate_act = jnp.einsum(
        "hcsd,df->hcsf", group_rows, gate_weight, preferred_element_type=jnp.float32
    )
    up_act = jnp.einsum(
        "hcsd,df->hcsf", group_rows, up_weight, preferred_element_type=jnp.float32
    )
    hidden = (jax.nn.silu(gate_act) * up_act).astype(jnp.bfloat16)
    partial_out = jnp.einsum(
        "hcsf,df->hcsd", hidden, down_weight, preferred_element_type=jnp.float32
    ).astype(jnp.bfloat16)
    shard_out = jnp.swapaxes(
        lax.psum_scatter(partial_out, "head", scatter_dimension=0, tiled=False), 0, 1
    )
    returned = lax.all_to_all(shard_out, "seq", split_axis=0, concat_axis=0, tiled=True)
    by_expert = returned.reshape(expert_count, replicas, CAP, D)
    first_hot = (slot_ids[:, 0, None, None] == slot_grid[None]).astype(jnp.bfloat16)
    second_hot = (slot_ids[:, 1, None, None] == slot_grid[None]).astype(jnp.bfloat16)
    first_rows = jnp.sum(
        jnp.einsum("tec,ercd->trd", first_hot, by_expert, preferred_element_type=jnp.float32), 1
    )
    second_rows = jnp.sum(
        jnp.einsum("tec,ercd->trd", second_hot, by_expert, preferred_element_type=jnp.float32), 1
    )
    moe_sum = first_weight[:, None] * first_rows + second_weight[:, None] * second_rows
    residual_out = (middle_wide + residual_scale * moe_sum).astype(jnp.bfloat16)
    return (residual_out, key_head, value_head)


def solution(mesh):
    return jax.shard_map(
        per_device,
        mesh=mesh,
        in_specs=(
            P(("seq", "head"), None),
            P(("seq", "head"), None),
            P(("seq", "head"), None),
            P(("seq", "head"), None),
            P(),
            P(),
            P("seq"),
            P(("seq", "head"), None),
            P(None, ("seq", "head")),
            P(None, ("seq", "head")),
            P(None, ("seq", "head")),
            P("head", None),
        ),
        out_specs=(P(("seq", "head"), None), P("seq", "head"), P("seq", "head")),
        check_vma=False,
    )
```

```python
import math

import jax
import jax.numpy as jnp
from jax import lax
from jax.experimental import pallas as pl
from jax.experimental.pallas import tpu as pltpu
from jax.experimental.layout import Layout, with_layout_constraint
from jax.sharding import PartitionSpec as P

D = 2304
HDIM = 64
LEVELS = 4
CAP = 9


residual_scale = 1.4 / math.sqrt(40.0)
norm_epsilon = 1e-05


def passed_along(value, axis, by):
    length = lax.axis_size(axis)
    pairs = [(i, i + by) for i in range(length) if 0 <= i + by < length]
    return lax.ppermute(value, axis, pairs)


def score_piece(queries, key_piece, piece_allowed):
    raw_scores = jnp.einsum(
        "qhd,hdk->hqk", queries, key_piece, preferred_element_type=jnp.float32
    ) * queries.shape[2] ** (-0.5)
    return jnp.where(piece_allowed[None], raw_scores, -jnp.inf)


def mix_piece(rounded_piece, value_piece):
    return jnp.einsum(
        "hqk,hdk->qhd", rounded_piece, value_piece, preferred_element_type=jnp.float32
    )


def attention_project(q3, window_t, allowed, out_weight):
    heads, tokens, _ = q3.shape
    key_total = window_t.shape[1]
    width = out_weight.shape[1]

    def kernel(q_ref, keys_ref, values_ref, allowed_ref, weight_ref, out_ref, total_ref):
        head = pl.program_id(0)

        @pl.when(head == 0)
        def _():
            total_ref[...] = jnp.zeros(total_ref.shape, jnp.float32)

        allowed_now = allowed_ref[...] != 0
        raw = jnp.dot(q_ref[0], keys_ref[...], preferred_element_type=jnp.float32) * HDIM ** (-0.5)
        masked = jnp.where(allowed_now, raw, -jnp.inf)
        top = jnp.max(masked, axis=1, keepdims=True)
        weights = jnp.where(allowed_now, jnp.exp(masked - top), 0.0)
        sums = jnp.sum(weights, axis=1, keepdims=True)
        mixed = lax.dot_general(
            weights.astype(jnp.bfloat16), values_ref[...], (((1,), (1,)), ((), ())),
            preferred_element_type=jnp.float32)
        attended = (mixed / sums).astype(jnp.bfloat16)
        total_ref[...] += jnp.dot(attended, weight_ref[...], preferred_element_type=jnp.float32)

        @pl.when(head == heads - 1)
        def _():
            out_ref[...] = total_ref[...].astype(out_ref.dtype)

    return pl.pallas_call(
        kernel,
        grid=(heads,),
        in_specs=[
            pl.BlockSpec((1, tokens, HDIM), lambda h: (h, 0, 0)),
            pl.BlockSpec((HDIM, key_total), lambda h: (h, 0)),
            pl.BlockSpec((HDIM, key_total), lambda h: (h + heads, 0)),
            pl.BlockSpec((tokens, key_total), lambda h: (0, 0)),
            pl.BlockSpec((HDIM, width), lambda h: (h, 0)),
        ],
        out_specs=pl.BlockSpec((tokens, width), lambda h: (0, 0)),
        out_shape=jax.ShapeDtypeStruct((tokens, width), jnp.bfloat16),
        scratch_shapes=[pltpu.VMEM((tokens, width), jnp.float32)],
        compiler_params=pltpu.CompilerParams(dimension_semantics=("arbitrary",)),
    )(q3, window_t, window_t, allowed.astype(jnp.int32), out_weight)


def per_device(
    query_rows,
    key_rows,
    value_rows,
    residual_in,
    norm_gain,
    router_weight,
    segment_ids,
    expert_ids,
    gate_weight,
    up_weight,
    down_weight,
    out_weight,
):
    head_count = lax.axis_size("head")
    seq_count = lax.axis_size("seq")
    tok_local = query_rows.shape[0]
    group_width = query_rows.shape[1] // head_count
    heads_here = group_width // HDIM
    stretch_len = tok_local * head_count
    span_count = min(2**LEVELS * 32 // tok_local, seq_count)
    expert_count = router_weight.shape[1]
    replicas = seq_count // expert_count
    seq_place = lax.axis_index("seq")
    joined_rows_t = jnp.concatenate(
        (
            jnp.transpose(key_rows).reshape(head_count, group_width, tok_local),
            jnp.transpose(value_rows).reshape(head_count, group_width, tok_local),
        ),
        1,
    )
    joined_head_t = lax.all_to_all(
        joined_rows_t, "head", split_axis=0, concat_axis=2, tiled=True
    ).reshape(2 * group_width, stretch_len)
    joined_head_t = with_layout_constraint(joined_head_t, Layout(major_to_minor=(0, 1)))
    key_head = jnp.transpose(joined_head_t[:group_width])
    value_head = jnp.transpose(joined_head_t[group_width:])
    query_head = lax.all_to_all(
        query_rows.reshape(tok_local, head_count, group_width),
        "head",
        split_axis=1,
        concat_axis=0,
        tiled=True,
    ).reshape(stretch_len, group_width)
    all_segments = lax.all_gather(segment_ids, "seq", axis=0, tiled=True)
    if span_count == seq_count:
        joined_window_t = lax.all_gather(joined_head_t, "seq", axis=1, tiled=True)
        segment_window = all_segments
        window_first = 0
    else:
        pieces = [joined_head_t]
        for distance in range(1, span_count):
            pieces.append(passed_along(joined_head_t, "seq", distance))
        joined_window_t = jnp.concatenate(pieces[::-1], 1)
        front_rows = (span_count - 1) * stretch_len
        segment_window = lax.dynamic_slice_in_dim(
            jnp.concatenate((jnp.zeros((front_rows,), jnp.int32), all_segments), 0),
            seq_place * stretch_len,
            span_count * stretch_len,
            0,
        )
        window_first = (seq_place - span_count + 1) * stretch_len
    key_total = span_count * stretch_len
    joined_window_t = with_layout_constraint(joined_window_t, Layout(major_to_minor=(0, 1)))
    query_place = seq_place * stretch_len + jnp.arange(stretch_len, dtype=jnp.int32)
    key_place = window_first + jnp.arange(key_total, dtype=jnp.int32)
    allowed = (
        (segment_window[None, :] == segment_ids[:, None])
        & (key_place[None, :] <= query_place[:, None])
        & (key_place[None, :] >= 0)
    )
    queries = jnp.transpose(query_head.reshape(stretch_len, heads_here, HDIM), (1, 0, 2))
    attended_sum = lax.psum_scatter(
        attention_project(queries, joined_window_t, allowed, out_weight),
        "head",
        scatter_dimension=0,
        tiled=True,
    ).astype(jnp.float32)
    middle = (residual_in.astype(jnp.float32) + residual_scale * attended_sum).astype(jnp.bfloat16)
    middle_wide = middle.astype(jnp.float32)
    mean_square = jnp.mean(middle_wide * middle_wide, -1, keepdims=True)
    normed = (middle_wide * lax.rsqrt(mean_square + norm_epsilon) * norm_gain).astype(jnp.bfloat16)
    route_count = expert_ids.shape[1]
    logits = jnp.dot(normed, router_weight, preferred_element_type=jnp.float32)
    route_hot = expert_ids[:, :, None] == jnp.arange(expert_count, dtype=jnp.int32)[None, None, :]
    chosen = jnp.sum(jnp.where(route_hot, logits[:, None, :], 0.0), -1)
    first_weight = 1.0 / (1.0 + jnp.exp(chosen[:, 1] - chosen[:, 0]))
    second_weight = 1.0 / (1.0 + jnp.exp(chosen[:, 0] - chosen[:, 1]))
    flat_hot = route_hot.reshape(tok_local * route_count, expert_count).astype(jnp.int32)
    before_count = jnp.cumsum(flat_hot, 0) - flat_hot
    route_rank = jnp.sum(before_count * flat_hot, -1)
    slot_ids = (expert_ids.reshape(-1) * CAP + route_rank).reshape(tok_local, route_count)
    slot_total = expert_count * CAP
    slot_grid = jnp.arange(slot_total, dtype=jnp.int32).reshape(expert_count, CAP)
    dispatch = jnp.any(
        slot_ids[None, None, :, :] == slot_grid[:, :, None, None], -1
    ).astype(jnp.bfloat16)
    packed = jnp.einsum(
        "ect,td->ecd", dispatch, normed, preferred_element_type=jnp.float32
    ).astype(jnp.bfloat16)
    outgoing = jnp.broadcast_to(packed[:, None], (expert_count, replicas, CAP, D)).reshape(
        seq_count, CAP, D
    )
    arrived = lax.all_to_all(outgoing, "seq", split_axis=0, concat_axis=0, tiled=True)
    group_rows = lax.all_gather(jnp.swapaxes(arrived, 0, 1), "head", axis=0, tiled=False)
    gate_act = jnp.einsum(
        "hcsd,df->hcsf", group_rows, gate_weight, preferred_element_type=jnp.float32
    )
    up_act = jnp.einsum(
        "hcsd,df->hcsf", group_rows, up_weight, preferred_element_type=jnp.float32
    )
    hidden = (jax.nn.silu(gate_act) * up_act).astype(jnp.bfloat16)
    partial_out = jnp.einsum(
        "hcsf,df->hcsd", hidden, down_weight, preferred_element_type=jnp.float32
    ).astype(jnp.bfloat16)
    shard_out = jnp.swapaxes(
        lax.psum_scatter(partial_out, "head", scatter_dimension=0, tiled=False), 0, 1
    )
    returned = lax.all_to_all(shard_out, "seq", split_axis=0, concat_axis=0, tiled=True)
    by_expert = returned.reshape(expert_count, replicas, CAP, D)
    first_hot = (slot_ids[:, 0, None, None] == slot_grid[None]).astype(jnp.bfloat16)
    second_hot = (slot_ids[:, 1, None, None] == slot_grid[None]).astype(jnp.bfloat16)
    first_rows = jnp.sum(
        jnp.einsum("tec,ercd->trd", first_hot, by_expert, preferred_element_type=jnp.float32), 1
    )
    second_rows = jnp.sum(
        jnp.einsum("tec,ercd->trd", second_hot, by_expert, preferred_element_type=jnp.float32), 1
    )
    moe_sum = first_weight[:, None] * first_rows + second_weight[:, None] * second_rows
    residual_out = (middle_wide + residual_scale * moe_sum).astype(jnp.bfloat16)
    return (residual_out, key_head, value_head)


def solution(mesh):
    return jax.shard_map(
        per_device,
        mesh=mesh,
        in_specs=(
            P(("seq", "head"), None),
            P(("seq", "head"), None),
            P(("seq", "head"), None),
            P(("seq", "head"), None),
            P(),
            P(),
            P("seq"),
            P(("seq", "head"), None),
            P(None, ("seq", "head")),
            P(None, ("seq", "head")),
            P(None, ("seq", "head")),
            P("head", None),
        ),
        out_specs=(P(("seq", "head"), None), P("seq", "head"), P("seq", "head")),
        check_vma=False,
    )
```

```python
import math

import jax
import jax.numpy as jnp
from jax import lax
from jax.experimental import pallas as pl
from jax.experimental.layout import Layout, with_layout_constraint
from jax.sharding import PartitionSpec as P

D = 2304
HDIM = 64
LEVELS = 4
CAP = 9


residual_scale = 1.4 / math.sqrt(40.0)
norm_epsilon = 1e-05


def passed_along(value, axis, by):
    length = lax.axis_size(axis)
    pairs = [(i, i + by) for i in range(length) if 0 <= i + by < length]
    return lax.ppermute(value, axis, pairs)


def score_piece(queries, key_piece, piece_allowed):
    raw_scores = jnp.einsum(
        "qhd,hdk->hqk", queries, key_piece, preferred_element_type=jnp.float32
    ) * queries.shape[2] ** (-0.5)
    return jnp.where(piece_allowed[None], raw_scores, -jnp.inf)


def mix_piece(rounded_piece, value_piece):
    return jnp.einsum(
        "hqk,hdk->qhd", rounded_piece, value_piece, preferred_element_type=jnp.float32
    )


def attention_project(q3, window_t, allowed, out_weight):
    heads, tokens, _ = q3.shape
    group_width = heads * HDIM

    def kernel(q_ref, window_ref, allowed_ref, weight_ref, out_ref):
        allowed_now = allowed_ref[...] != 0
        total = jnp.zeros(out_ref.shape, jnp.float32)
        for head in range(heads):
            keys = window_ref[pl.ds(head * HDIM, HDIM), :]
            values = window_ref[pl.ds(group_width + head * HDIM, HDIM), :]
            raw = jnp.dot(q_ref[head], keys, preferred_element_type=jnp.float32) * HDIM ** (-0.5)
            masked = jnp.where(allowed_now, raw, -jnp.inf)
            top = jnp.max(masked, axis=1, keepdims=True)
            weights = jnp.exp(masked - top)
            sums = jnp.sum(weights, axis=1, keepdims=True)
            mixed = lax.dot_general(
                weights.astype(jnp.bfloat16),
                values,
                (((1,), (1,)), ((), ())),
                preferred_element_type=jnp.float32,
            )
            attended = (mixed / sums).astype(jnp.bfloat16)
            total = total + jnp.dot(
                attended,
                weight_ref[pl.ds(head * HDIM, HDIM), :],
                preferred_element_type=jnp.float32,
            )
        out_ref[...] = total.astype(out_ref.dtype)

    return pl.pallas_call(
        kernel, out_shape=jax.ShapeDtypeStruct((tokens, out_weight.shape[1]), jnp.bfloat16)
    )(q3, window_t, allowed.astype(jnp.int32), out_weight)


def per_device(
    query_rows,
    key_rows,
    value_rows,
    residual_in,
    norm_gain,
    router_weight,
    segment_ids,
    expert_ids,
    gate_weight,
    up_weight,
    down_weight,
    out_weight,
):
    head_count = lax.axis_size("head")
    seq_count = lax.axis_size("seq")
    tok_local = query_rows.shape[0]
    group_width = query_rows.shape[1] // head_count
    heads_here = group_width // HDIM
    stretch_len = tok_local * head_count
    span_count = min(2**LEVELS * 32 // tok_local, seq_count)
    expert_count = router_weight.shape[1]
    replicas = seq_count // expert_count
    seq_place = lax.axis_index("seq")
    joined_rows_t = jnp.concatenate(
        (
            jnp.transpose(key_rows).reshape(head_count, group_width, tok_local),
            jnp.transpose(value_rows).reshape(head_count, group_width, tok_local),
        ),
        1,
    )
    joined_head_t = lax.all_to_all(
        joined_rows_t, "head", split_axis=0, concat_axis=2, tiled=True
    ).reshape(2 * group_width, stretch_len)
    joined_head_t = with_layout_constraint(joined_head_t, Layout(major_to_minor=(0, 1)))
    key_head = jnp.transpose(joined_head_t[:group_width])
    value_head = jnp.transpose(joined_head_t[group_width:])
    query_head = lax.all_to_all(
        query_rows.reshape(tok_local, head_count, group_width),
        "head",
        split_axis=1,
        concat_axis=0,
        tiled=True,
    ).reshape(stretch_len, group_width)
    all_segments = lax.all_gather(segment_ids, "seq", axis=0, tiled=True)
    if span_count == seq_count:
        joined_window_t = lax.all_gather(joined_head_t, "seq", axis=1, tiled=True)
        segment_window = all_segments
        window_first = 0
    else:
        pieces = [joined_head_t]
        for distance in range(1, span_count):
            pieces.append(passed_along(joined_head_t, "seq", distance))
        joined_window_t = jnp.concatenate(pieces[::-1], 1)
        front_rows = (span_count - 1) * stretch_len
        segment_window = lax.dynamic_slice_in_dim(
            jnp.concatenate((jnp.zeros((front_rows,), jnp.int32), all_segments), 0),
            seq_place * stretch_len,
            span_count * stretch_len,
            0,
        )
        window_first = (seq_place - span_count + 1) * stretch_len
    key_total = span_count * stretch_len
    joined_window_t = with_layout_constraint(joined_window_t, Layout(major_to_minor=(0, 1)))
    query_place = seq_place * stretch_len + jnp.arange(stretch_len, dtype=jnp.int32)
    key_place = window_first + jnp.arange(key_total, dtype=jnp.int32)
    allowed = (
        (segment_window[None, :] == segment_ids[:, None])
        & (key_place[None, :] <= query_place[:, None])
        & (key_place[None, :] >= 0)
    )
    queries = jnp.transpose(query_head.reshape(stretch_len, heads_here, HDIM), (1, 0, 2))
    attended_sum = lax.psum_scatter(
        attention_project(queries, joined_window_t, allowed, out_weight),
        "head",
        scatter_dimension=0,
        tiled=True,
    ).astype(jnp.float32)
    middle = (residual_in.astype(jnp.float32) + residual_scale * attended_sum).astype(jnp.bfloat16)
    middle_wide = middle.astype(jnp.float32)
    mean_square = jnp.mean(middle_wide * middle_wide, -1, keepdims=True)
    normed = (middle_wide * lax.rsqrt(mean_square + norm_epsilon) * norm_gain).astype(jnp.bfloat16)
    route_count = expert_ids.shape[1]
    logits = jnp.dot(normed, router_weight, preferred_element_type=jnp.float32)
    route_hot = expert_ids[:, :, None] == jnp.arange(expert_count, dtype=jnp.int32)[None, None, :]
    chosen = jnp.sum(jnp.where(route_hot, logits[:, None, :], 0.0), -1)
    first_weight = 1.0 / (1.0 + jnp.exp(chosen[:, 1] - chosen[:, 0]))
    second_weight = 1.0 / (1.0 + jnp.exp(chosen[:, 0] - chosen[:, 1]))
    flat_hot = route_hot.reshape(tok_local * route_count, expert_count).astype(jnp.int32)
    before_count = jnp.cumsum(flat_hot, 0) - flat_hot
    route_rank = jnp.sum(before_count * flat_hot, -1)
    slot_ids = (expert_ids.reshape(-1) * CAP + route_rank).reshape(tok_local, route_count)
    slot_total = expert_count * CAP
    slot_grid = jnp.arange(slot_total, dtype=jnp.int32).reshape(expert_count, CAP)
    dispatch = jnp.any(
        slot_ids[None, None, :, :] == slot_grid[:, :, None, None], -1
    ).astype(jnp.bfloat16)
    packed = jnp.einsum(
        "ect,td->ecd", dispatch, normed, preferred_element_type=jnp.float32
    ).astype(jnp.bfloat16)
    outgoing = jnp.broadcast_to(packed[:, None], (expert_count, replicas, CAP, D)).reshape(
        seq_count, CAP, D
    )
    arrived = lax.all_to_all(outgoing, "seq", split_axis=0, concat_axis=0, tiled=True)
    group_rows = lax.all_gather(jnp.swapaxes(arrived, 0, 1), "head", axis=0, tiled=False)
    gate_act = jnp.einsum(
        "hcsd,df->hcsf", group_rows, gate_weight, preferred_element_type=jnp.float32
    )
    up_act = jnp.einsum(
        "hcsd,df->hcsf", group_rows, up_weight, preferred_element_type=jnp.float32
    )
    hidden = (jax.nn.silu(gate_act) * up_act).astype(jnp.bfloat16)
    partial_out = jnp.einsum(
        "hcsf,df->hcsd", hidden, down_weight, preferred_element_type=jnp.float32
    ).astype(jnp.bfloat16)
    shard_out = jnp.swapaxes(
        lax.psum_scatter(partial_out, "head", scatter_dimension=0, tiled=False), 0, 1
    )
    returned = lax.all_to_all(shard_out, "seq", split_axis=0, concat_axis=0, tiled=True)
    by_expert = returned.reshape(expert_count, replicas, CAP, D)
    first_hot = (slot_ids[:, 0, None, None] == slot_grid[None]).astype(jnp.bfloat16)
    second_hot = (slot_ids[:, 1, None, None] == slot_grid[None]).astype(jnp.bfloat16)
    first_rows = jnp.sum(
        jnp.einsum("tec,ercd->trd", first_hot, by_expert, preferred_element_type=jnp.float32), 1
    )
    second_rows = jnp.sum(
        jnp.einsum("tec,ercd->trd", second_hot, by_expert, preferred_element_type=jnp.float32), 1
    )
    moe_sum = first_weight[:, None] * first_rows + second_weight[:, None] * second_rows
    residual_out = (middle_wide + residual_scale * moe_sum).astype(jnp.bfloat16)
    return (residual_out, key_head, value_head)


def solution(mesh):
    return jax.shard_map(
        per_device,
        mesh=mesh,
        in_specs=(
            P(("seq", "head"), None),
            P(("seq", "head"), None),
            P(("seq", "head"), None),
            P(("seq", "head"), None),
            P(),
            P(),
            P("seq"),
            P(("seq", "head"), None),
            P(None, ("seq", "head")),
            P(None, ("seq", "head")),
            P(None, ("seq", "head")),
            P("head", None),
        ),
        out_specs=(P(("seq", "head"), None), P("seq", "head"), P("seq", "head")),
        check_vma=False,
    )
```

```python
import math

import jax
import jax.numpy as jnp
from jax import lax
from jax.experimental import pallas as pl
from jax.experimental.pallas import tpu as pltpu
from jax.experimental.layout import Layout, with_layout_constraint
from jax.sharding import PartitionSpec as P

D = 2304
HDIM = 64
LEVELS = 4
CAP = 9


residual_scale = 1.4 / math.sqrt(40.0)
norm_epsilon = 1e-05


def passed_along(value, axis, by):
    length = lax.axis_size(axis)
    pairs = [(i, i + by) for i in range(length) if 0 <= i + by < length]
    return lax.ppermute(value, axis, pairs)


def score_piece(queries, key_piece, piece_allowed):
    raw_scores = jnp.einsum(
        "qhd,hdk->hqk", queries, key_piece, preferred_element_type=jnp.float32
    ) * queries.shape[2] ** (-0.5)
    return jnp.where(piece_allowed[None], raw_scores, -jnp.inf)


def mix_piece(rounded_piece, value_piece):
    return jnp.einsum(
        "hqk,hdk->qhd", rounded_piece, value_piece, preferred_element_type=jnp.float32
    )


def attention_project(q3, window_t, allowed, out_weight):
    heads, tokens, _ = q3.shape
    group_width = heads * HDIM

    def kernel(q_ref, window_ref, allowed_ref, weight_ref, out_ref, gathered_ref):
        allowed_now = allowed_ref[...] != 0
        for head in range(heads):
            keys = window_ref[pl.ds(head * HDIM, HDIM), :]
            values = window_ref[pl.ds(group_width + head * HDIM, HDIM), :]
            raw = jnp.dot(q_ref[head], keys, preferred_element_type=jnp.float32) * HDIM ** (-0.5)
            masked = jnp.where(allowed_now, raw, -jnp.inf)
            top = jnp.max(masked, axis=1, keepdims=True)
            weights = jnp.exp(masked - top)
            sums = jnp.sum(weights, axis=1, keepdims=True)
            mixed = lax.dot_general(
                weights.astype(jnp.bfloat16),
                values,
                (((1,), (1,)), ((), ())),
                preferred_element_type=jnp.float32,
            )
            attended = (mixed / sums).astype(jnp.bfloat16).astype(jnp.float32)
            gathered_ref[pl.ds(head * HDIM, HDIM), :] = jnp.transpose(attended).astype(
                jnp.bfloat16
            )
        out_ref[...] = lax.dot_general(
            gathered_ref[...],
            weight_ref[...],
            (((0,), (0,)), ((), ())),
            preferred_element_type=jnp.float32,
        ).astype(out_ref.dtype)

    return pl.pallas_call(
        kernel,
        out_shape=jax.ShapeDtypeStruct((tokens, out_weight.shape[1]), jnp.bfloat16),
        scratch_shapes=[pltpu.VMEM((group_width, tokens), jnp.bfloat16)],
    )(q3, window_t, allowed.astype(jnp.int32), out_weight)


def per_device(
    query_rows,
    key_rows,
    value_rows,
    residual_in,
    norm_gain,
    router_weight,
    segment_ids,
    expert_ids,
    gate_weight,
    up_weight,
    down_weight,
    out_weight,
):
    head_count = lax.axis_size("head")
    seq_count = lax.axis_size("seq")
    tok_local = query_rows.shape[0]
    group_width = query_rows.shape[1] // head_count
    heads_here = group_width // HDIM
    stretch_len = tok_local * head_count
    span_count = min(2**LEVELS * 32 // tok_local, seq_count)
    expert_count = router_weight.shape[1]
    replicas = seq_count // expert_count
    seq_place = lax.axis_index("seq")
    joined_rows_t = jnp.concatenate(
        (
            jnp.transpose(key_rows).reshape(head_count, group_width, tok_local),
            jnp.transpose(value_rows).reshape(head_count, group_width, tok_local),
        ),
        1,
    )
    joined_head_t = lax.all_to_all(
        joined_rows_t, "head", split_axis=0, concat_axis=2, tiled=True
    ).reshape(2 * group_width, stretch_len)
    joined_head_t = with_layout_constraint(joined_head_t, Layout(major_to_minor=(0, 1)))
    key_head = jnp.transpose(joined_head_t[:group_width])
    value_head = jnp.transpose(joined_head_t[group_width:])
    query_head = lax.all_to_all(
        query_rows.reshape(tok_local, head_count, group_width),
        "head",
        split_axis=1,
        concat_axis=0,
        tiled=True,
    ).reshape(stretch_len, group_width)
    all_segments = lax.all_gather(segment_ids, "seq", axis=0, tiled=True)
    if span_count == seq_count:
        joined_window_t = lax.all_gather(joined_head_t, "seq", axis=1, tiled=True)
        segment_window = all_segments
        window_first = 0
    else:
        pieces = [joined_head_t]
        for distance in range(1, span_count):
            pieces.append(passed_along(joined_head_t, "seq", distance))
        joined_window_t = jnp.concatenate(pieces[::-1], 1)
        front_rows = (span_count - 1) * stretch_len
        segment_window = lax.dynamic_slice_in_dim(
            jnp.concatenate((jnp.zeros((front_rows,), jnp.int32), all_segments), 0),
            seq_place * stretch_len,
            span_count * stretch_len,
            0,
        )
        window_first = (seq_place - span_count + 1) * stretch_len
    key_total = span_count * stretch_len
    joined_window_t = with_layout_constraint(joined_window_t, Layout(major_to_minor=(0, 1)))
    query_place = seq_place * stretch_len + jnp.arange(stretch_len, dtype=jnp.int32)
    key_place = window_first + jnp.arange(key_total, dtype=jnp.int32)
    allowed = (
        (segment_window[None, :] == segment_ids[:, None])
        & (key_place[None, :] <= query_place[:, None])
        & (key_place[None, :] >= 0)
    )
    queries = jnp.transpose(query_head.reshape(stretch_len, heads_here, HDIM), (1, 0, 2))
    attended_sum = lax.psum_scatter(
        attention_project(queries, joined_window_t, allowed, out_weight),
        "head",
        scatter_dimension=0,
        tiled=True,
    ).astype(jnp.float32)
    middle = (residual_in.astype(jnp.float32) + residual_scale * attended_sum).astype(jnp.bfloat16)
    middle_wide = middle.astype(jnp.float32)
    mean_square = jnp.mean(middle_wide * middle_wide, -1, keepdims=True)
    normed = (middle_wide * lax.rsqrt(mean_square + norm_epsilon) * norm_gain).astype(jnp.bfloat16)
    route_count = expert_ids.shape[1]
    logits = jnp.dot(normed, router_weight, preferred_element_type=jnp.float32)
    route_hot = expert_ids[:, :, None] == jnp.arange(expert_count, dtype=jnp.int32)[None, None, :]
    chosen = jnp.sum(jnp.where(route_hot, logits[:, None, :], 0.0), -1)
    first_weight = 1.0 / (1.0 + jnp.exp(chosen[:, 1] - chosen[:, 0]))
    second_weight = 1.0 / (1.0 + jnp.exp(chosen[:, 0] - chosen[:, 1]))
    flat_hot = route_hot.reshape(tok_local * route_count, expert_count).astype(jnp.int32)
    before_count = jnp.cumsum(flat_hot, 0) - flat_hot
    route_rank = jnp.sum(before_count * flat_hot, -1)
    slot_ids = (expert_ids.reshape(-1) * CAP + route_rank).reshape(tok_local, route_count)
    slot_total = expert_count * CAP
    slot_grid = jnp.arange(slot_total, dtype=jnp.int32).reshape(expert_count, CAP)
    dispatch = jnp.any(
        slot_ids[None, None, :, :] == slot_grid[:, :, None, None], -1
    ).astype(jnp.bfloat16)
    packed = jnp.einsum(
        "ect,td->ecd", dispatch, normed, preferred_element_type=jnp.float32
    ).astype(jnp.bfloat16)
    outgoing = jnp.broadcast_to(packed[:, None], (expert_count, replicas, CAP, D)).reshape(
        seq_count, CAP, D
    )
    arrived = lax.all_to_all(outgoing, "seq", split_axis=0, concat_axis=0, tiled=True)
    group_rows = lax.all_gather(jnp.swapaxes(arrived, 0, 1), "head", axis=0, tiled=False)
    gate_act = jnp.einsum(
        "hcsd,df->hcsf", group_rows, gate_weight, preferred_element_type=jnp.float32
    )
    up_act = jnp.einsum(
        "hcsd,df->hcsf", group_rows, up_weight, preferred_element_type=jnp.float32
    )
    hidden = (jax.nn.silu(gate_act) * up_act).astype(jnp.bfloat16)
    partial_out = jnp.einsum(
        "hcsf,df->hcsd", hidden, down_weight, preferred_element_type=jnp.float32
    ).astype(jnp.bfloat16)
    shard_out = jnp.swapaxes(
        lax.psum_scatter(partial_out, "head", scatter_dimension=0, tiled=False), 0, 1
    )
    returned = lax.all_to_all(shard_out, "seq", split_axis=0, concat_axis=0, tiled=True)
    by_expert = returned.reshape(expert_count, replicas, CAP, D)
    first_hot = (slot_ids[:, 0, None, None] == slot_grid[None]).astype(jnp.bfloat16)
    second_hot = (slot_ids[:, 1, None, None] == slot_grid[None]).astype(jnp.bfloat16)
    first_rows = jnp.sum(
        jnp.einsum("tec,ercd->trd", first_hot, by_expert, preferred_element_type=jnp.float32), 1
    )
    second_rows = jnp.sum(
        jnp.einsum("tec,ercd->trd", second_hot, by_expert, preferred_element_type=jnp.float32), 1
    )
    moe_sum = first_weight[:, None] * first_rows + second_weight[:, None] * second_rows
    residual_out = (middle_wide + residual_scale * moe_sum).astype(jnp.bfloat16)
    return (residual_out, key_head, value_head)


def solution(mesh):
    return jax.shard_map(
        per_device,
        mesh=mesh,
        in_specs=(
            P(("seq", "head"), None),
            P(("seq", "head"), None),
            P(("seq", "head"), None),
            P(("seq", "head"), None),
            P(),
            P(),
            P("seq"),
            P(("seq", "head"), None),
            P(None, ("seq", "head")),
            P(None, ("seq", "head")),
            P(None, ("seq", "head")),
            P("head", None),
        ),
        out_specs=(P(("seq", "head"), None), P("seq", "head"), P("seq", "head")),
        check_vma=False,
    )
```

```python
import math

import jax
import jax.numpy as jnp
from jax import lax
from jax.experimental import pallas as pl
from jax.experimental.pallas import tpu as pltpu
from jax.experimental.layout import Layout, with_layout_constraint
from jax.sharding import PartitionSpec as P

D = 2304
HDIM = 64
LEVELS = 4
CAP = 9


residual_scale = 1.4 / math.sqrt(40.0)
norm_epsilon = 1e-05


def passed_along(value, axis, by):
    length = lax.axis_size(axis)
    pairs = [(i, i + by) for i in range(length) if 0 <= i + by < length]
    return lax.ppermute(value, axis, pairs)


def score_piece(queries, key_piece, piece_allowed):
    raw_scores = jnp.einsum(
        "qhd,hdk->hqk", queries, key_piece, preferred_element_type=jnp.float32
    ) * queries.shape[2] ** (-0.5)
    return jnp.where(piece_allowed[None], raw_scores, -jnp.inf)


def mix_piece(rounded_piece, value_piece):
    return jnp.einsum(
        "hqk,hdk->qhd", rounded_piece, value_piece, preferred_element_type=jnp.float32
    )


def attention_project(q3, window_t, allowed, out_weight):
    heads, tokens, _ = q3.shape
    group_width = heads * HDIM

    def kernel(q_ref, window_ref, allowed_ref, weight_ref, out_ref, gathered_ref):
        allowed_now = allowed_ref[...] != 0
        for head in range(heads):
            keys = window_ref[pl.ds(head * HDIM, HDIM), :]
            values = window_ref[pl.ds(group_width + head * HDIM, HDIM), :]
            raw = lax.dot_general(
                keys,
                q_ref[head],
                (((0,), (1,)), ((), ())),
                preferred_element_type=jnp.float32,
            ) * HDIM ** (-0.5)
            masked = jnp.where(allowed_now, raw, -jnp.inf)
            top = jnp.max(masked, axis=0, keepdims=True)
            weights = jnp.exp(masked - top)
            sums = jnp.sum(weights, axis=0, keepdims=True)
            mixed = jnp.dot(values, weights.astype(jnp.bfloat16), preferred_element_type=jnp.float32)
            gathered_ref[pl.ds(head * HDIM, HDIM), :] = (mixed / sums).astype(jnp.bfloat16)
        out_ref[...] = lax.dot_general(
            gathered_ref[...],
            weight_ref[...],
            (((0,), (0,)), ((), ())),
            preferred_element_type=jnp.float32,
        ).astype(out_ref.dtype)

    return pl.pallas_call(
        kernel,
        out_shape=jax.ShapeDtypeStruct((tokens, out_weight.shape[1]), jnp.bfloat16),
        scratch_shapes=[pltpu.VMEM((group_width, tokens), jnp.bfloat16)],
    )(q3, window_t, jnp.transpose(allowed).astype(jnp.int32), out_weight)


def per_device(
    query_rows,
    key_rows,
    value_rows,
    residual_in,
    norm_gain,
    router_weight,
    segment_ids,
    expert_ids,
    gate_weight,
    up_weight,
    down_weight,
    out_weight,
):
    head_count = lax.axis_size("head")
    seq_count = lax.axis_size("seq")
    tok_local = query_rows.shape[0]
    group_width = query_rows.shape[1] // head_count
    heads_here = group_width // HDIM
    stretch_len = tok_local * head_count
    span_count = min(2**LEVELS * 32 // tok_local, seq_count)
    expert_count = router_weight.shape[1]
    replicas = seq_count // expert_count
    seq_place = lax.axis_index("seq")
    joined_rows_t = jnp.concatenate(
        (
            jnp.transpose(key_rows).reshape(head_count, group_width, tok_local),
            jnp.transpose(value_rows).reshape(head_count, group_width, tok_local),
        ),
        1,
    )
    joined_head_t = lax.all_to_all(
        joined_rows_t, "head", split_axis=0, concat_axis=2, tiled=True
    ).reshape(2 * group_width, stretch_len)
    joined_head_t = with_layout_constraint(joined_head_t, Layout(major_to_minor=(0, 1)))
    key_head = jnp.transpose(joined_head_t[:group_width])
    value_head = jnp.transpose(joined_head_t[group_width:])
    query_head = lax.all_to_all(
        query_rows.reshape(tok_local, head_count, group_width),
        "head",
        split_axis=1,
        concat_axis=0,
        tiled=True,
    ).reshape(stretch_len, group_width)
    all_segments = lax.all_gather(segment_ids, "seq", axis=0, tiled=True)
    if span_count == seq_count:
        joined_window_t = lax.all_gather(joined_head_t, "seq", axis=1, tiled=True)
        segment_window = all_segments
        window_first = 0
    else:
        pieces = [joined_head_t]
        for distance in range(1, span_count):
            pieces.append(passed_along(joined_head_t, "seq", distance))
        joined_window_t = jnp.concatenate(pieces[::-1], 1)
        front_rows = (span_count - 1) * stretch_len
        segment_window = lax.dynamic_slice_in_dim(
            jnp.concatenate((jnp.zeros((front_rows,), jnp.int32), all_segments), 0),
            seq_place * stretch_len,
            span_count * stretch_len,
            0,
        )
        window_first = (seq_place - span_count + 1) * stretch_len
    key_total = span_count * stretch_len
    joined_window_t = with_layout_constraint(joined_window_t, Layout(major_to_minor=(0, 1)))
    query_place = seq_place * stretch_len + jnp.arange(stretch_len, dtype=jnp.int32)
    key_place = window_first + jnp.arange(key_total, dtype=jnp.int32)
    allowed = (
        (segment_window[None, :] == segment_ids[:, None])
        & (key_place[None, :] <= query_place[:, None])
        & (key_place[None, :] >= 0)
    )
    queries = jnp.transpose(query_head.reshape(stretch_len, heads_here, HDIM), (1, 0, 2))
    attended_sum = lax.psum_scatter(
        attention_project(queries, joined_window_t, allowed, out_weight),
        "head",
        scatter_dimension=0,
        tiled=True,
    ).astype(jnp.float32)
    middle = (residual_in.astype(jnp.float32) + residual_scale * attended_sum).astype(jnp.bfloat16)
    middle_wide = middle.astype(jnp.float32)
    mean_square = jnp.mean(middle_wide * middle_wide, -1, keepdims=True)
    normed = (middle_wide * lax.rsqrt(mean_square + norm_epsilon) * norm_gain).astype(jnp.bfloat16)
    route_count = expert_ids.shape[1]
    logits = jnp.dot(normed, router_weight, preferred_element_type=jnp.float32)
    route_hot = expert_ids[:, :, None] == jnp.arange(expert_count, dtype=jnp.int32)[None, None, :]
    chosen = jnp.sum(jnp.where(route_hot, logits[:, None, :], 0.0), -1)
    first_weight = 1.0 / (1.0 + jnp.exp(chosen[:, 1] - chosen[:, 0]))
    second_weight = 1.0 / (1.0 + jnp.exp(chosen[:, 0] - chosen[:, 1]))
    flat_hot = route_hot.reshape(tok_local * route_count, expert_count).astype(jnp.int32)
    before_count = jnp.cumsum(flat_hot, 0) - flat_hot
    route_rank = jnp.sum(before_count * flat_hot, -1)
    slot_ids = (expert_ids.reshape(-1) * CAP + route_rank).reshape(tok_local, route_count)
    slot_total = expert_count * CAP
    slot_grid = jnp.arange(slot_total, dtype=jnp.int32).reshape(expert_count, CAP)
    dispatch = jnp.any(
        slot_ids[None, None, :, :] == slot_grid[:, :, None, None], -1
    ).astype(jnp.bfloat16)
    packed = jnp.einsum(
        "ect,td->ecd", dispatch, normed, preferred_element_type=jnp.float32
    ).astype(jnp.bfloat16)
    outgoing = jnp.broadcast_to(packed[:, None], (expert_count, replicas, CAP, D)).reshape(
        seq_count, CAP, D
    )
    arrived = lax.all_to_all(outgoing, "seq", split_axis=0, concat_axis=0, tiled=True)
    group_rows = lax.all_gather(jnp.swapaxes(arrived, 0, 1), "head", axis=0, tiled=False)
    gate_act = jnp.einsum(
        "hcsd,df->hcsf", group_rows, gate_weight, preferred_element_type=jnp.float32
    )
    up_act = jnp.einsum(
        "hcsd,df->hcsf", group_rows, up_weight, preferred_element_type=jnp.float32
    )
    hidden = (jax.nn.silu(gate_act) * up_act).astype(jnp.bfloat16)
    partial_out = jnp.einsum(
        "hcsf,df->hcsd", hidden, down_weight, preferred_element_type=jnp.float32
    ).astype(jnp.bfloat16)
    shard_out = jnp.swapaxes(
        lax.psum_scatter(partial_out, "head", scatter_dimension=0, tiled=False), 0, 1
    )
    returned = lax.all_to_all(shard_out, "seq", split_axis=0, concat_axis=0, tiled=True)
    by_expert = returned.reshape(expert_count, replicas, CAP, D)
    first_hot = (slot_ids[:, 0, None, None] == slot_grid[None]).astype(jnp.bfloat16)
    second_hot = (slot_ids[:, 1, None, None] == slot_grid[None]).astype(jnp.bfloat16)
    first_rows = jnp.sum(
        jnp.einsum("tec,ercd->trd", first_hot, by_expert, preferred_element_type=jnp.float32), 1
    )
    second_rows = jnp.sum(
        jnp.einsum("tec,ercd->trd", second_hot, by_expert, preferred_element_type=jnp.float32), 1
    )
    moe_sum = first_weight[:, None] * first_rows + second_weight[:, None] * second_rows
    residual_out = (middle_wide + residual_scale * moe_sum).astype(jnp.bfloat16)
    return (residual_out, key_head, value_head)


def solution(mesh):
    return jax.shard_map(
        per_device,
        mesh=mesh,
        in_specs=(
            P(("seq", "head"), None),
            P(("seq", "head"), None),
            P(("seq", "head"), None),
            P(("seq", "head"), None),
            P(),
            P(),
            P("seq"),
            P(("seq", "head"), None),
            P(None, ("seq", "head")),
            P(None, ("seq", "head")),
            P(None, ("seq", "head")),
            P("head", None),
        ),
        out_specs=(P(("seq", "head"), None), P("seq", "head"), P("seq", "head")),
        check_vma=False,
    )
```

```python
import math

import jax
import jax.numpy as jnp
from jax import lax
from jax.experimental import pallas as pl
from jax.experimental.pallas import tpu as pltpu
from jax.experimental.layout import Layout, with_layout_constraint
from jax.sharding import PartitionSpec as P

D = 2304
HDIM = 64
LEVELS = 4
CAP = 9


residual_scale = 1.4 / math.sqrt(40.0)
norm_epsilon = 1e-05


def passed_along(value, axis, by):
    length = lax.axis_size(axis)
    pairs = [(i, i + by) for i in range(length) if 0 <= i + by < length]
    return lax.ppermute(value, axis, pairs)


def score_piece(queries, key_piece, piece_allowed):
    raw_scores = jnp.einsum(
        "qhd,hdk->hqk", queries, key_piece, preferred_element_type=jnp.float32
    ) * queries.shape[2] ** (-0.5)
    return jnp.where(piece_allowed[None], raw_scores, -jnp.inf)


def mix_piece(rounded_piece, value_piece):
    return jnp.einsum(
        "hqk,hdk->qhd", rounded_piece, value_piece, preferred_element_type=jnp.float32
    )


def attention_project(q3, window_t, query_info, key_info, out_weight):
    heads, tokens, _ = q3.shape
    group_width = heads * HDIM

    def kernel(q_ref, window_ref, query_ref, key_ref, weight_ref, out_ref, gathered_ref):
        query_now = query_ref[...]
        key_now = key_ref[...]
        allowed_now = (
            (key_now[0:1, :] == query_now[:, 0:1])
            & (key_now[1:2, :] <= query_now[:, 1:2])
            & (key_now[1:2, :] >= 0)
        )
        for head in range(heads):
            keys = window_ref[pl.ds(head * HDIM, HDIM), :]
            values = window_ref[pl.ds(group_width + head * HDIM, HDIM), :]
            raw = jnp.dot(q_ref[head], keys, preferred_element_type=jnp.float32) * HDIM ** (-0.5)
            masked = jnp.where(allowed_now, raw, -jnp.inf)
            top = jnp.max(masked, axis=1, keepdims=True)
            weights = jnp.exp(masked - top)
            sums = jnp.sum(weights, axis=1, keepdims=True)
            mixed = lax.dot_general(
                weights.astype(jnp.bfloat16),
                values,
                (((1,), (1,)), ((), ())),
                preferred_element_type=jnp.float32,
            )
            attended = (mixed / sums).astype(jnp.bfloat16).astype(jnp.float32)
            gathered_ref[pl.ds(head * HDIM, HDIM), :] = jnp.transpose(attended).astype(
                jnp.bfloat16
            )
        out_ref[...] = lax.dot_general(
            gathered_ref[...],
            weight_ref[...],
            (((0,), (0,)), ((), ())),
            preferred_element_type=jnp.float32,
        ).astype(out_ref.dtype)

    return pl.pallas_call(
        kernel,
        out_shape=jax.ShapeDtypeStruct((tokens, out_weight.shape[1]), jnp.bfloat16),
        scratch_shapes=[pltpu.VMEM((group_width, tokens), jnp.bfloat16)],
    )(q3, window_t, query_info, key_info, out_weight)


def per_device(
    query_rows,
    key_rows,
    value_rows,
    residual_in,
    norm_gain,
    router_weight,
    segment_ids,
    expert_ids,
    gate_weight,
    up_weight,
    down_weight,
    out_weight,
):
    head_count = lax.axis_size("head")
    seq_count = lax.axis_size("seq")
    tok_local = query_rows.shape[0]
    group_width = query_rows.shape[1] // head_count
    heads_here = group_width // HDIM
    stretch_len = tok_local * head_count
    span_count = min(2**LEVELS * 32 // tok_local, seq_count)
    expert_count = router_weight.shape[1]
    replicas = seq_count // expert_count
    seq_place = lax.axis_index("seq")
    joined_rows_t = jnp.concatenate(
        (
            jnp.transpose(key_rows).reshape(head_count, group_width, tok_local),
            jnp.transpose(value_rows).reshape(head_count, group_width, tok_local),
        ),
        1,
    )
    joined_head_t = lax.all_to_all(
        joined_rows_t, "head", split_axis=0, concat_axis=2, tiled=True
    ).reshape(2 * group_width, stretch_len)
    joined_head_t = with_layout_constraint(joined_head_t, Layout(major_to_minor=(0, 1)))
    key_head = jnp.transpose(joined_head_t[:group_width])
    value_head = jnp.transpose(joined_head_t[group_width:])
    query_head = lax.all_to_all(
        query_rows.reshape(tok_local, head_count, group_width),
        "head",
        split_axis=1,
        concat_axis=0,
        tiled=True,
    ).reshape(stretch_len, group_width)
    all_segments = lax.all_gather(segment_ids, "seq", axis=0, tiled=True)
    if span_count == seq_count:
        joined_window_t = lax.all_gather(joined_head_t, "seq", axis=1, tiled=True)
        segment_window = all_segments
        window_first = 0
    else:
        pieces = [joined_head_t]
        for distance in range(1, span_count):
            pieces.append(passed_along(joined_head_t, "seq", distance))
        joined_window_t = jnp.concatenate(pieces[::-1], 1)
        front_rows = (span_count - 1) * stretch_len
        segment_window = lax.dynamic_slice_in_dim(
            jnp.concatenate((jnp.zeros((front_rows,), jnp.int32), all_segments), 0),
            seq_place * stretch_len,
            span_count * stretch_len,
            0,
        )
        window_first = (seq_place - span_count + 1) * stretch_len
    key_total = span_count * stretch_len
    joined_window_t = with_layout_constraint(joined_window_t, Layout(major_to_minor=(0, 1)))
    query_place = seq_place * stretch_len + jnp.arange(stretch_len, dtype=jnp.int32)
    key_place = window_first + jnp.arange(key_total, dtype=jnp.int32)
    allowed = (
        (segment_window[None, :] == segment_ids[:, None])
        & (key_place[None, :] <= query_place[:, None])
        & (key_place[None, :] >= 0)
    )
    queries = jnp.transpose(query_head.reshape(stretch_len, heads_here, HDIM), (1, 0, 2))
    attended_sum = lax.psum_scatter(
        attention_project(
            queries,
            joined_window_t,
            jnp.stack((segment_ids, query_place), 1),
            jnp.stack((segment_window, key_place), 0),
            out_weight,
        ),
        "head",
        scatter_dimension=0,
        tiled=True,
    ).astype(jnp.float32)
    middle = (residual_in.astype(jnp.float32) + residual_scale * attended_sum).astype(jnp.bfloat16)
    middle_wide = middle.astype(jnp.float32)
    mean_square = jnp.mean(middle_wide * middle_wide, -1, keepdims=True)
    normed = (middle_wide * lax.rsqrt(mean_square + norm_epsilon) * norm_gain).astype(jnp.bfloat16)
    route_count = expert_ids.shape[1]
    logits = jnp.dot(normed, router_weight, preferred_element_type=jnp.float32)
    route_hot = expert_ids[:, :, None] == jnp.arange(expert_count, dtype=jnp.int32)[None, None, :]
    chosen = jnp.sum(jnp.where(route_hot, logits[:, None, :], 0.0), -1)
    first_weight = 1.0 / (1.0 + jnp.exp(chosen[:, 1] - chosen[:, 0]))
    second_weight = 1.0 / (1.0 + jnp.exp(chosen[:, 0] - chosen[:, 1]))
    flat_hot = route_hot.reshape(tok_local * route_count, expert_count).astype(jnp.int32)
    before_count = jnp.cumsum(flat_hot, 0) - flat_hot
    route_rank = jnp.sum(before_count * flat_hot, -1)
    slot_ids = (expert_ids.reshape(-1) * CAP + route_rank).reshape(tok_local, route_count)
    slot_total = expert_count * CAP
    slot_grid = jnp.arange(slot_total, dtype=jnp.int32).reshape(expert_count, CAP)
    dispatch = jnp.any(
        slot_ids[None, None, :, :] == slot_grid[:, :, None, None], -1
    ).astype(jnp.bfloat16)
    packed = jnp.einsum(
        "ect,td->ecd", dispatch, normed, preferred_element_type=jnp.float32
    ).astype(jnp.bfloat16)
    outgoing = jnp.broadcast_to(packed[:, None], (expert_count, replicas, CAP, D)).reshape(
        seq_count, CAP, D
    )
    arrived = lax.all_to_all(outgoing, "seq", split_axis=0, concat_axis=0, tiled=True)
    group_rows = lax.all_gather(jnp.swapaxes(arrived, 0, 1), "head", axis=0, tiled=False)
    gate_act = jnp.einsum(
        "hcsd,df->hcsf", group_rows, gate_weight, preferred_element_type=jnp.float32
    )
    up_act = jnp.einsum(
        "hcsd,df->hcsf", group_rows, up_weight, preferred_element_type=jnp.float32
    )
    hidden = (jax.nn.silu(gate_act) * up_act).astype(jnp.bfloat16)
    partial_out = jnp.einsum(
        "hcsf,df->hcsd", hidden, down_weight, preferred_element_type=jnp.float32
    ).astype(jnp.bfloat16)
    shard_out = jnp.swapaxes(
        lax.psum_scatter(partial_out, "head", scatter_dimension=0, tiled=False), 0, 1
    )
    returned = lax.all_to_all(shard_out, "seq", split_axis=0, concat_axis=0, tiled=True)
    by_expert = returned.reshape(expert_count, replicas, CAP, D)
    first_hot = (slot_ids[:, 0, None, None] == slot_grid[None]).astype(jnp.bfloat16)
    second_hot = (slot_ids[:, 1, None, None] == slot_grid[None]).astype(jnp.bfloat16)
    first_rows = jnp.sum(
        jnp.einsum("tec,ercd->trd", first_hot, by_expert, preferred_element_type=jnp.float32), 1
    )
    second_rows = jnp.sum(
        jnp.einsum("tec,ercd->trd", second_hot, by_expert, preferred_element_type=jnp.float32), 1
    )
    moe_sum = first_weight[:, None] * first_rows + second_weight[:, None] * second_rows
    residual_out = (middle_wide + residual_scale * moe_sum).astype(jnp.bfloat16)
    return (residual_out, key_head, value_head)


def solution(mesh):
    return jax.shard_map(
        per_device,
        mesh=mesh,
        in_specs=(
            P(("seq", "head"), None),
            P(("seq", "head"), None),
            P(("seq", "head"), None),
            P(("seq", "head"), None),
            P(),
            P(),
            P("seq"),
            P(("seq", "head"), None),
            P(None, ("seq", "head")),
            P(None, ("seq", "head")),
            P(None, ("seq", "head")),
            P("head", None),
        ),
        out_specs=(P(("seq", "head"), None), P("seq", "head"), P("seq", "head")),
        check_vma=False,
    )
```
